128 devices in a mesh: visit: 4 (over x), patch: 32 (over y, z, core).
Axes of the slice: x: 4, y: 4, z: 4, core: 2. Of those that a mesh axis runs over, the one named last changes fastest.
Arguments:
- pixels: bfloat16 [8192, 128, 128], P(('visit', 'patch')), may hold values from -6 to 6
- mask_bits: int32 [8192, 128, 128], P(('visit', 'patch')), may hold values from 0 to 15, as said below
- inv_var: float32 [8192], P(('visit', 'patch')), may hold values from 0.05 to 1
- owner: int32 [8192], P(('visit', 'patch')), may hold values from 0 to 31, as said below
- cell: int32 [8192], P(('visit', 'patch')), may hold values from 0 to 63
- coef_index: int32 [8192], P(('visit', 'patch')), may hold values from 0 to 63
- coef_table: float32 [64, 9], replicated, may hold values from -4 to 4
Outputs:
- coadd: float32 [2048, 128, 128], P('patch', 'visit')
- difference: bfloat16 [8192, 128, 128], P(('visit', 'patch'))
The draws below stay inside these ranges and needn't reach their ends.
Inputs may be any that keep to these rules, and one draw needn't show every extreme that they name: `owner`: within each device's 64 blocks (aligned runs of 64 in order) no patch is named more than 8 times; one patch, the same for all devices, is named exactly 8 times in every such run. `mask_bits`: each value is a sum of the bit flags 1, 2, 4 and 8.
All inputs are finite; a program needn't handle non-finite values.
Results may differ from the reference program's by a relative error of at most 0.0071.
Values may be sent and summed in bfloat16 or wider, within the bound.
No kernel may reach another device: no remote copies, remote signals or barrier semaphores. Data moves between devices by JAX's collectives and lax.ppermute only.
A program may use at most 128 MiB of HBM per device.

```python
import math
import jax
import jax.numpy as jnp
from jax import lax

BP = 128
BLK_DEV = 64
CELLS = 64
KSIZE = 21
NBASIS = 9
NSET = 64
PATCHES = 32
CAP = 8
NBLK = 8192
N_PATCH = 32


def draw_owner(key, part):
    hot_patch = jax.random.randint(jax.random.fold_in(key, 11), (), 0, PATCHES).astype(jnp.int32)
    others = ((hot_patch + 1 + jnp.repeat(jnp.arange(PATCHES - 1), CAP)) % PATCHES).astype(jnp.int32)

    def one_device(device_key):
        first_key, second_key = jax.random.split(device_key)
        picked = jax.random.permutation(first_key, others)[:BLK_DEV - CAP]
        listing = jnp.concatenate([jnp.full((CAP,), hot_patch, jnp.int32), picked])
        return jax.random.permutation(second_key, listing)
    device_keys = jax.random.split(jax.random.fold_in(key, 13), NBLK // BLK_DEV)
    return jax.vmap(one_device)(device_keys).reshape(NBLK).astype(jnp.int32)


def draw_mask_bits(key, part):
    rolls = jax.random.randint(key, (NBLK, BP, BP), 0, 2 ** 24)
    bad_bit = (rolls % 64 < 4).astype(jnp.int32)
    saturated = (rolls // 64 % 64 < 2).astype(jnp.int32)
    cosmic_bit = (rolls // 4096 % 64 < 4).astype(jnp.int32)
    interpolated = (rolls // 262144 % 64 < 16).astype(jnp.int32)
    flags = bad_bit + 2 * saturated + 4 * cosmic_bit + 8 * interpolated
    return flags.at[0, 0, 0].set(15).at[0, 0, 1].set(0).astype(jnp.int32)


def plant(values, own_key, low, high):
    extent = values.shape
    spot = [jax.random.randint(jax.random.fold_in(own_key, axis), (), 0, extent[axis]) for axis in range(len(extent))]
    values = values.at[tuple(spot)].set(low)
    longest = extent.index(max(extent))
    spot[longest] = (spot[longest] + 1) % extent[longest]
    return values.at[tuple(spot)].set(high)


def block_scale(key, shape, shards, low, top_value):
    def one(axis_at, blocks):
        heights = jax.random.uniform(jax.random.fold_in(jax.random.fold_in(key, 6), axis_at), (blocks,), jnp.float32, low / len(shards), top_value / len(shards))
        return jnp.repeat(jnp.exp(heights), shape[axis_at] // blocks).reshape((-1,) + (1,) * (len(shape) - axis_at - 1))

    factor_of = one(*shards[0])
    for cut in shards[1:]:
        factor_of = factor_of * one(*cut)
    return factor_of


def normal_values(key, extent, scale, bound, pieces=(), held_as=jnp.bfloat16):
    values = jax.random.normal(key, extent, jnp.float32) * scale
    if len(pieces) > 0:
        values = block_scale(key, extent, pieces, -0.22, 0.18) * values
    return jnp.clip(values, min=-bound, max=bound).astype(held_as)


def setup_inputs(seed: int = 0) -> dict:
    arg_keys = jax.random.split(jax.random.key(seed), 8)
    pixels = normal_values(arg_keys[0], (NBLK, BP, BP), 1.0, 6.0, ((0, 128),))
    mask_bits = draw_mask_bits(jax.random.fold_in(arg_keys[7], 71), 0)
    inv_var = jnp.clip(jnp.exp(math.log(1.0) - 2.9957323 * jax.random.uniform(arg_keys[2], (NBLK,), jnp.float32) ** block_scale(arg_keys[2], (NBLK,), ((0, 128),), -0.2, 0.2)), 0.05, 1.0)
    owner = draw_owner(jax.random.fold_in(arg_keys[7], 71), 0)
    cell = plant(jax.random.randint(arg_keys[4], (NBLK,), 0, CELLS), jax.random.fold_in(arg_keys[4], 1), 0, CELLS - 1).astype(jnp.int32)
    coef_index = plant(jax.random.randint(arg_keys[5], (NBLK,), 0, NSET), jax.random.fold_in(arg_keys[5], 1), 0, NSET - 1).astype(jnp.int32)
    coef_table = normal_values(arg_keys[6], (NSET, NBASIS), 0.7, 4.0, (), jnp.float32)
    return {"pixels": pixels, "mask_bits": mask_bits, "inv_var": inv_var, "owner": owner, "cell": cell, "coef_index": coef_index, "coef_table": coef_table}


gauss_widths = (1.0, 2.0, 3.5)


def band_tables(side_len):
    tap_reach = KSIZE // 2
    position = jnp.arange(side_len).astype(jnp.float32)
    offset = position[:, None] - position[None, :]
    inside = jnp.abs(offset) <= tap_reach
    tap_offsets = jnp.arange(-tap_reach, tap_reach + 1).astype(jnp.float32)
    tables = []
    for spread in gauss_widths:
        profile_sum = jnp.sum(jnp.exp(-tap_offsets * tap_offsets / (2.0 * spread * spread)))
        even_band = jnp.where(inside, jnp.exp(-offset * offset / (2.0 * spread * spread)) / profile_sum, 0.0)
        tables.append(even_band)
        tables.append(even_band * offset / spread)
    return jnp.stack(tables)


def match_group(blocks, coefficients, tables, right_bands):
    number = blocks.shape[0]
    side_len = blocks.shape[1]
    columns = jnp.dot(blocks.reshape(number * side_len, side_len), right_bands, preferred_element_type=jnp.float32)
    columns = columns.astype(jnp.bfloat16).reshape(number, side_len, 6, side_len)
    left_parts = []
    for sigma_pos in range(3):
        even_band = tables[2 * sigma_pos]
        odd_band = tables[2 * sigma_pos + 1]
        left_parts.append(coefficients[:, 3 * sigma_pos, None, None] * even_band + coefficients[:, 3 * sigma_pos + 1, None, None] * odd_band)
        left_parts.append(coefficients[:, 3 * sigma_pos + 2, None, None] * even_band)
    left_bands = jnp.stack(left_parts, axis=2).astype(jnp.bfloat16)
    result = jnp.einsum("nisp,npsj->nij", left_bands.astype(jnp.float32), columns.astype(jnp.float32))
    return result.astype(jnp.bfloat16)


def reference(pixels, mask_bits, inv_var, owner, cell, coef_index, coef_table):
    number = pixels.shape[0]
    side_len = pixels.shape[1]
    tables = band_tables(side_len)
    right_bands = jnp.transpose(tables, (2, 0, 1)).reshape(side_len, 6 * side_len).astype(jnp.bfloat16)
    usable = (mask_bits % 2 == 0) & ((mask_bits // 2) % 2 == 0) & ((mask_bits // 4) % 2 == 0)
    masked = jnp.where(usable, pixels, jnp.zeros((), jnp.bfloat16))
    chosen = (coef_index[:, None] == jnp.arange(NSET).astype(jnp.int32)[None, :]).astype(jnp.float32)
    coefficients = jnp.dot(chosen, coef_table, precision=lax.Precision.HIGHEST)
    rounds = number // 64

    def one_batch(bundle):
        return match_group(bundle[0], bundle[1], tables, right_bands)

    matched = lax.map(one_batch, (masked.reshape(rounds, 64, side_len, side_len), coefficients.reshape(rounds, 64, NBASIS)))
    matched = matched.reshape(number, side_len, side_len)
    weight = lax.optimization_barrier(inv_var.astype(jnp.bfloat16)).astype(jnp.float32)
    segment = (owner * CELLS + cell).astype(jnp.int32)
    numerator = jax.ops.segment_sum(weight[:, None, None] * matched.astype(jnp.float32), segment, num_segments=N_PATCH * CELLS)
    weight_sum = jax.ops.segment_sum(weight, segment, num_segments=N_PATCH * CELLS)
    coadd = numerator / jnp.maximum(weight_sum, 1.0)[:, None, None]
    template = coadd.astype(jnp.bfloat16)
    difference = (matched.astype(jnp.float32) - template[segment].astype(jnp.float32)).astype(jnp.bfloat16)
    return coadd, difference
```

```python
import functools

import jax
import jax.numpy as jnp
from jax import lax
from jax.experimental import pallas as pl
from jax.experimental.pallas import tpu as pltpu
from jax.sharding import PartitionSpec as P

CELLS = 64
KSIZE = 21
GROUP = 8


gauss_widths = (1.0, 2.0, 3.5)


def band_tables(side_len):
    tap_reach = KSIZE // 2
    position = jnp.arange(side_len).astype(jnp.float32)
    offset = position[:, None] - position[None, :]
    inside = jnp.abs(offset) <= tap_reach
    tap_offsets = jnp.arange(-tap_reach, tap_reach + 1).astype(jnp.float32)
    tables = []
    for spread in gauss_widths:
        profile_sum = jnp.sum(jnp.exp(-tap_offsets * tap_offsets / (2.0 * spread * spread)))
        even_band = jnp.where(
            inside, jnp.exp(-offset * offset / (2.0 * spread * spread)) / profile_sum, 0.0
        )
        tables.append(even_band)
        tables.append(even_band * offset / spread)
    return jnp.stack(tables)


def match_kernel(coef_ref, pix_ref, mask_ref, tab_ref, right_ref, out_ref):
    step = pl.program_id(0)
    group, side_len, _ = pix_ref.shape
    bits = mask_ref[...]
    masked = jnp.where((bits & 7) == 0, pix_ref[...], jnp.zeros((), jnp.bfloat16))
    columns = jnp.dot(
        masked.reshape(group * side_len, side_len),
        right_ref[...],
        preferred_element_type=jnp.float32,
    ).astype(jnp.bfloat16)
    for g in range(group):
        base = (step * group + g) * 9
        rows = columns[g * side_len:(g + 1) * side_len]
        acc = jnp.zeros((side_len, side_len), jnp.float32)
        for m in range(3):
            even_band = tab_ref[2 * m]
            odd_band = tab_ref[2 * m + 1]
            left_a = (coef_ref[base + 3 * m] * even_band
                      + coef_ref[base + 3 * m + 1] * odd_band).astype(jnp.bfloat16)
            left_b = (coef_ref[base + 3 * m + 2] * even_band).astype(jnp.bfloat16)
            acc = acc + jnp.dot(
                left_a, rows[:, (2 * m) * side_len:(2 * m + 1) * side_len],
                preferred_element_type=jnp.float32,
            )
            acc = acc + jnp.dot(
                left_b, rows[:, (2 * m + 1) * side_len:(2 * m + 2) * side_len],
                preferred_element_type=jnp.float32,
            )
        out_ref[g] = acc.astype(jnp.bfloat16)


def match_blocks(pixels, mask_bits, coefficients, tables, right_bands):
    number, side_len, _ = pixels.shape
    steps = number // GROUP
    flops = number * 4 * side_len * side_len * 6 * side_len
    return pl.pallas_call(
        match_kernel,
        out_shape=jax.ShapeDtypeStruct(pixels.shape, jnp.bfloat16),
        grid=(steps,),
        in_specs=[
            pl.BlockSpec(memory_space=pltpu.SMEM),
            pl.BlockSpec((GROUP, side_len, side_len), lambda i: (i, 0, 0)),
            pl.BlockSpec((GROUP, side_len, side_len), lambda i: (i, 0, 0)),
            pl.BlockSpec(tables.shape, lambda i: (0, 0, 0)),
            pl.BlockSpec(right_bands.shape, lambda i: (0, 0)),
        ],
        out_specs=pl.BlockSpec((GROUP, side_len, side_len), lambda i: (i, 0, 0)),
        cost_estimate=pl.CostEstimate(
            flops=flops, transcendentals=0, bytes_accessed=number * side_len * side_len * 8
        ),
    )(coefficients.reshape(-1), pixels, mask_bits, tables, right_bands)


def shards(pixels, mask_bits, inv_var, owner, cell, coef_index, coef_table):
    blocks_here = pixels.shape[0]
    side_len = pixels.shape[1]
    patches = lax.axis_size("patch")
    visits = lax.axis_size("visit")
    capacity = 4 * blocks_here // patches
    slot_total = patches * capacity
    tables = band_tables(side_len)
    right_bands = (
        jnp.transpose(tables, (2, 0, 1)).reshape(side_len, 6 * side_len).astype(jnp.bfloat16)
    )
    coefficients = coef_table[coef_index]
    matched_home = match_blocks(pixels, mask_bits, coefficients, tables, right_bands)
    weight = inv_var.astype(jnp.bfloat16)
    cell_weight = jnp.where(
        cell[:, None] == jnp.arange(CELLS)[None, :], weight[:, None], jnp.zeros((), jnp.bfloat16)
    )
    dest_onehot = (owner[:, None] == jnp.arange(patches)[None, :]).astype(jnp.int32)
    slot_rank = jnp.sum((jnp.cumsum(dest_onehot, axis=0) - dest_onehot) * dest_onehot, axis=1)
    slot_of_block = owner * capacity + slot_rank
    matches = slot_of_block[None, :] == jnp.arange(slot_total)[:, None]
    source_row = jnp.sum(jnp.where(matches, jnp.arange(blocks_here)[None, :], 0), axis=1)
    filled = jnp.any(matches, axis=1)

    def pack_slots(values):
        picked = values[source_row]
        keep_rows = filled.reshape((slot_total,) + (1,) * (values.ndim - 1))
        picked = jnp.where(keep_rows, picked, jnp.zeros((), values.dtype))
        return picked.reshape((patches, capacity) + values.shape[1:])

    pieces = lax.all_to_all(
        pack_slots(matched_home), "patch", split_axis=0, concat_axis=0, tiled=True
    )
    weights = lax.all_to_all(
        pack_slots(cell_weight), "patch", split_axis=0, concat_axis=0, tiled=True
    )
    flat_weights = weights.reshape(slot_total, CELLS)
    flat_matched = pieces.reshape(slot_total, side_len * side_len)
    numerator = jnp.einsum(
        "sc,sk->ck", flat_weights, flat_matched, preferred_element_type=jnp.float32
    ).reshape(CELLS, side_len, side_len)
    weight_sum = jnp.sum(flat_weights.astype(jnp.float32), axis=0)
    numerator_part = lax.psum_scatter(numerator, "visit", scatter_dimension=1, tiled=True)
    weight_sum = lax.psum(weight_sum, "visit")
    coadd_part = numerator_part / jnp.maximum(weight_sum, 1.0)[:, None, None]
    template = lax.all_gather(coadd_part.astype(jnp.bfloat16), "visit", axis=1, tiled=True)
    live_slots = (flat_weights > 0).astype(jnp.bfloat16)
    slot_template = jnp.einsum(
        "sc,ck->sk",
        live_slots,
        template.reshape(CELLS, side_len * side_len),
        preferred_element_type=jnp.float32,
    )
    difference_slots = (flat_matched.astype(jnp.float32) - slot_template).astype(jnp.bfloat16)
    returned = lax.all_to_all(
        difference_slots.reshape(patches, capacity, side_len, side_len),
        "patch",
        split_axis=0,
        concat_axis=0,
        tiled=True,
    )
    difference = returned.reshape(slot_total, side_len, side_len)[slot_of_block]
    return (coadd_part, difference)


def solution(mesh):
    placed = (
        P(("visit", "patch"), None, None),
        P(("visit", "patch"), None, None),
        P(("visit", "patch")),
        P(("visit", "patch")),
        P(("visit", "patch")),
        P(("visit", "patch")),
        P(),
    )
    return jax.shard_map(
        shards,
        mesh=mesh,
        in_specs=placed,
        out_specs=(P("patch", "visit", None), P(("visit", "patch"), None, None)),
        check_vma=False,
    )
```

```python
import functools

import jax
import jax.numpy as jnp
from jax import lax
from jax.experimental import pallas as pl
from jax.experimental.pallas import tpu as pltpu
from jax.sharding import PartitionSpec as P

CELLS = 64
KSIZE = 21
GROUP = 8


gauss_widths = (1.0, 2.0, 3.5)


def band_tables(side_len):
    tap_reach = KSIZE // 2
    position = jnp.arange(side_len).astype(jnp.float32)
    offset = position[:, None] - position[None, :]
    inside = jnp.abs(offset) <= tap_reach
    tap_offsets = jnp.arange(-tap_reach, tap_reach + 1).astype(jnp.float32)
    tables = []
    for spread in gauss_widths:
        profile_sum = jnp.sum(jnp.exp(-tap_offsets * tap_offsets / (2.0 * spread * spread)))
        even_band = jnp.where(
            inside, jnp.exp(-offset * offset / (2.0 * spread * spread)) / profile_sum, 0.0
        )
        tables.append(even_band)
        tables.append(even_band * offset / spread)
    return jnp.stack(tables)


def match_kernel(coef_ref, pix_ref, mask_ref, tab_ref, right_ref, out_ref):
    step = pl.program_id(0)
    group, side_len, _ = pix_ref.shape
    bits = mask_ref[...]
    masked = jnp.where((bits & 7) == 0, pix_ref[...], jnp.zeros((), jnp.bfloat16))
    columns = jnp.dot(
        masked.reshape(group * side_len, side_len),
        right_ref[...],
        preferred_element_type=jnp.float32,
    ).astype(jnp.bfloat16)
    for g in range(group):
        base = (step * group + g) * 9
        rows = columns[g * side_len:(g + 1) * side_len]
        acc = jnp.zeros((side_len, side_len), jnp.float32)
        for m in range(3):
            even_band = tab_ref[2 * m]
            odd_band = tab_ref[2 * m + 1]
            left_a = (coef_ref[base + 3 * m] * even_band
                      + coef_ref[base + 3 * m + 1] * odd_band).astype(jnp.bfloat16)
            left_b = (coef_ref[base + 3 * m + 2] * even_band).astype(jnp.bfloat16)
            acc = acc + jnp.dot(
                left_a, rows[:, (2 * m) * side_len:(2 * m + 1) * side_len],
                preferred_element_type=jnp.float32,
            )
            acc = acc + jnp.dot(
                left_b, rows[:, (2 * m + 1) * side_len:(2 * m + 2) * side_len],
                preferred_element_type=jnp.float32,
            )
        out_ref[g] = acc.astype(jnp.bfloat16)


def match_blocks(pixels, mask_bits, coefficients, tables, right_bands):
    number, side_len, _ = pixels.shape
    steps = number // GROUP
    flops = number * 4 * side_len * side_len * 6 * side_len
    return pl.pallas_call(
        match_kernel,
        out_shape=jax.ShapeDtypeStruct(pixels.shape, jnp.bfloat16),
        grid=(steps,),
        in_specs=[
            pl.BlockSpec(memory_space=pltpu.SMEM),
            pl.BlockSpec((GROUP, side_len, side_len), lambda i: (i, 0, 0)),
            pl.BlockSpec((GROUP, side_len, side_len), lambda i: (i, 0, 0)),
            pl.BlockSpec(tables.shape, lambda i: (0, 0, 0)),
            pl.BlockSpec(right_bands.shape, lambda i: (0, 0)),
        ],
        out_specs=pl.BlockSpec((GROUP, side_len, side_len), lambda i: (i, 0, 0)),
        cost_estimate=pl.CostEstimate(
            flops=flops, transcendentals=0, bytes_accessed=number * side_len * side_len * 8
        ),
    )(coefficients.reshape(-1), pixels, mask_bits, tables, right_bands)


def shards(pixels, mask_bits, inv_var, owner, cell, coef_index, coef_table):
    blocks_here = pixels.shape[0]
    side_len = pixels.shape[1]
    patches = lax.axis_size("patch")
    visits = lax.axis_size("visit")
    devices = patches * visits
    segments = patches * CELLS
    rows_here = side_len // visits
    both = ("visit", "patch")
    tables = band_tables(side_len)
    right_bands = (
        jnp.transpose(tables, (2, 0, 1)).reshape(side_len, 6 * side_len).astype(jnp.bfloat16)
    )
    coefficients = coef_table[coef_index]
    matched_home = match_blocks(pixels, mask_bits, coefficients, tables, right_bands)
    by_row = jnp.transpose(matched_home, (1, 0, 2))
    row_all = lax.all_to_all(by_row, both, split_axis=0, concat_axis=0, tiled=True)
    row_all = row_all.reshape(devices * blocks_here, side_len)
    weight_all = lax.all_gather(inv_var.astype(jnp.bfloat16), both, tiled=True)
    segment_all = lax.all_gather((owner * CELLS + cell).astype(jnp.int32), both, tiled=True)
    picks = segment_all[None, :] == jnp.arange(segments, dtype=jnp.int32)[:, None]
    weighted = jnp.where(picks, weight_all[None, :], jnp.zeros((), jnp.bfloat16))
    numerator = jnp.dot(weighted, row_all, preferred_element_type=jnp.float32)
    weight_sum = jnp.sum(weighted.astype(jnp.float32), axis=1)
    coadd_row = numerator / jnp.maximum(weight_sum, 1.0)[:, None]
    template_row = coadd_row.astype(jnp.bfloat16)
    difference_row = (
        row_all.astype(jnp.float32) - template_row[segment_all].astype(jnp.float32)
    ).astype(jnp.bfloat16)
    returned = lax.all_to_all(
        difference_row.reshape(devices, blocks_here, side_len),
        both, split_axis=0, concat_axis=0, tiled=True,
    )
    difference = jnp.transpose(returned, (1, 0, 2))
    coadd_parts = lax.all_to_all(
        coadd_row.reshape(patches, CELLS, 1, side_len),
        "patch", split_axis=0, concat_axis=2, tiled=True,
    )
    coadd_part = coadd_parts.reshape(CELLS, rows_here, side_len)
    return (coadd_part, difference)


def solution(mesh):
    placed = (
        P(("visit", "patch"), None, None),
        P(("visit", "patch"), None, None),
        P(("visit", "patch")),
        P(("visit", "patch")),
        P(("visit", "patch")),
        P(("visit", "patch")),
        P(),
    )
    return jax.shard_map(
        shards,
        mesh=mesh,
        in_specs=placed,
        out_specs=(P("patch", "visit", None), P(("visit", "patch"), None, None)),
        check_vma=False,
    )
```

```python
import functools

import jax
import jax.numpy as jnp
from jax import lax
from jax.experimental import pallas as pl
from jax.experimental.pallas import tpu as pltpu
from jax.sharding import PartitionSpec as P

CELLS = 64
KSIZE = 21
GROUP = 8


gauss_widths = (1.0, 2.0, 3.5)


def band_tables(side_len):
    tap_reach = KSIZE // 2
    position = jnp.arange(side_len).astype(jnp.float32)
    offset = position[:, None] - position[None, :]
    inside = jnp.abs(offset) <= tap_reach
    tap_offsets = jnp.arange(-tap_reach, tap_reach + 1).astype(jnp.float32)
    tables = []
    for spread in gauss_widths:
        profile_sum = jnp.sum(jnp.exp(-tap_offsets * tap_offsets / (2.0 * spread * spread)))
        even_band = jnp.where(
            inside, jnp.exp(-offset * offset / (2.0 * spread * spread)) / profile_sum, 0.0
        )
        tables.append(even_band)
        tables.append(even_band * offset / spread)
    return jnp.stack(tables)


def match_kernel(coef_ref, pix_ref, mask_ref, tab_ref, right_ref, out_ref):
    step = pl.program_id(0)
    group, side_len, _ = pix_ref.shape
    bits = mask_ref[...]
    masked = jnp.where((bits & 7) == 0, pix_ref[...], jnp.zeros((), jnp.bfloat16))
    columns = jnp.dot(
        masked.reshape(group * side_len, side_len),
        right_ref[...],
        preferred_element_type=jnp.float32,
    ).astype(jnp.bfloat16)
    for g in range(group):
        base = (step * group + g) * 9
        rows = columns[g * side_len:(g + 1) * side_len]
        acc = jnp.zeros((side_len, side_len), jnp.float32)
        for m in range(3):
            even_band = tab_ref[2 * m]
            odd_band = tab_ref[2 * m + 1]
            left_a = (coef_ref[base + 3 * m] * even_band
                      + coef_ref[base + 3 * m + 1] * odd_band).astype(jnp.bfloat16)
            left_b = (coef_ref[base + 3 * m + 2] * even_band).astype(jnp.bfloat16)
            acc = acc + jnp.dot(
                left_a, rows[:, (2 * m) * side_len:(2 * m + 1) * side_len],
                preferred_element_type=jnp.float32,
            )
            acc = acc + jnp.dot(
                left_b, rows[:, (2 * m + 1) * side_len:(2 * m + 2) * side_len],
                preferred_element_type=jnp.float32,
            )
        out_ref[g] = acc.astype(jnp.bfloat16)


def match_blocks(pixels, mask_bits, coefficients, tables, right_bands):
    number, side_len, _ = pixels.shape
    steps = number // GROUP
    flops = number * 4 * side_len * side_len * 6 * side_len
    return pl.pallas_call(
        match_kernel,
        out_shape=jax.ShapeDtypeStruct(pixels.shape, jnp.bfloat16),
        grid=(steps,),
        in_specs=[
            pl.BlockSpec(memory_space=pltpu.SMEM),
            pl.BlockSpec((GROUP, side_len, side_len), lambda i: (i, 0, 0)),
            pl.BlockSpec((GROUP, side_len, side_len), lambda i: (i, 0, 0)),
            pl.BlockSpec(tables.shape, lambda i: (0, 0, 0)),
            pl.BlockSpec(right_bands.shape, lambda i: (0, 0)),
        ],
        out_specs=pl.BlockSpec((GROUP, side_len, side_len), lambda i: (i, 0, 0)),
        cost_estimate=pl.CostEstimate(
            flops=flops, transcendentals=0, bytes_accessed=number * side_len * side_len * 8
        ),
    )(coefficients.reshape(-1), pixels, mask_bits, tables, right_bands)


def shards(pixels, mask_bits, inv_var, owner, cell, coef_index, coef_table):
    blocks_here = pixels.shape[0]
    side_len = pixels.shape[1]
    patches = lax.axis_size("patch")
    visits = lax.axis_size("visit")
    devices = patches * visits
    segments = patches * CELLS
    rows_here = side_len // visits
    both = ("visit", "patch")
    tables = band_tables(side_len)
    right_bands = (
        jnp.transpose(tables, (2, 0, 1)).reshape(side_len, 6 * side_len).astype(jnp.bfloat16)
    )
    coefficients = coef_table[coef_index]
    matched_home = match_blocks(pixels, mask_bits, coefficients, tables, right_bands)
    by_row = jnp.transpose(matched_home, (1, 0, 2))
    row_all = lax.all_to_all(by_row, both, split_axis=0, concat_axis=0, tiled=True)
    row_all = row_all.reshape(devices * blocks_here, side_len)
    meta = jnp.stack([
        inv_var.astype(jnp.bfloat16).astype(jnp.float32),
        owner.astype(jnp.float32),
        cell.astype(jnp.float32),
    ])
    meta = jnp.pad(meta, ((0, 8 - meta.shape[0]), (0, side_len - blocks_here)))
    meta_all = lax.all_gather(meta, both, axis=0, tiled=True).reshape(devices, 8, side_len)
    weight_all = meta_all[:, 0, :blocks_here].reshape(-1).astype(jnp.bfloat16)
    owner_all = meta_all[:, 1, :blocks_here].reshape(-1).astype(jnp.int32)
    cell_all = meta_all[:, 2, :blocks_here].reshape(-1).astype(jnp.int32)
    segment_all = owner_all * CELLS + cell_all
    picks = segment_all[None, :] == jnp.arange(segments, dtype=jnp.int32)[:, None]
    weighted = jnp.where(picks, weight_all[None, :], jnp.zeros((), jnp.bfloat16))
    numerator = jnp.dot(weighted, row_all, preferred_element_type=jnp.float32)
    owner_pick = (owner_all[None, :] == jnp.arange(patches, dtype=jnp.int32)[:, None]).astype(
        jnp.bfloat16
    )
    cell_pick = jnp.where(
        cell_all[None, :] == jnp.arange(CELLS, dtype=jnp.int32)[:, None],
        weight_all[None, :],
        jnp.zeros((), jnp.bfloat16),
    )
    weight_sum = lax.dot_general(
        owner_pick, cell_pick, (((1,), (1,)), ((), ())), preferred_element_type=jnp.float32
    ).reshape(segments)
    coadd_row = numerator / jnp.maximum(weight_sum, 1.0)[:, None]
    template_row = coadd_row.astype(jnp.bfloat16)
    block_pick = (
        segment_all[:, None] == jnp.arange(segments, dtype=jnp.int32)[None, :]
    ).astype(jnp.bfloat16)
    block_template = jnp.dot(block_pick, template_row, preferred_element_type=jnp.float32)
    difference_row = (row_all.astype(jnp.float32) - block_template).astype(jnp.bfloat16)
    returned = lax.all_to_all(
        difference_row.reshape(devices, blocks_here, side_len),
        both, split_axis=0, concat_axis=0, tiled=True,
    )
    difference = jnp.transpose(returned, (1, 0, 2))
    coadd_parts = lax.all_to_all(
        coadd_row.reshape(patches, CELLS, 1, side_len),
        "patch", split_axis=0, concat_axis=2, tiled=True,
    )
    coadd_part = coadd_parts.reshape(CELLS, rows_here, side_len)
    return (coadd_part, difference)


def solution(mesh):
    placed = (
        P(("visit", "patch"), None, None),
        P(("visit", "patch"), None, None),
        P(("visit", "patch")),
        P(("visit", "patch")),
        P(("visit", "patch")),
        P(("visit", "patch")),
        P(),
    )
    return jax.shard_map(
        shards,
        mesh=mesh,
        in_specs=placed,
        out_specs=(P("patch", "visit", None), P(("visit", "patch"), None, None)),
        check_vma=False,
    )
```

```python
import functools

import jax
import jax.numpy as jnp
from jax import lax
from jax.experimental import pallas as pl
from jax.experimental.pallas import tpu as pltpu
from jax.sharding import PartitionSpec as P

CELLS = 64
KSIZE = 21
GROUP = 8


gauss_widths = (1.0, 2.0, 3.5)


def band_tables(side_len):
    tap_reach = KSIZE // 2
    position = jnp.arange(side_len).astype(jnp.float32)
    offset = position[:, None] - position[None, :]
    inside = jnp.abs(offset) <= tap_reach
    tap_offsets = jnp.arange(-tap_reach, tap_reach + 1).astype(jnp.float32)
    tables = []
    for spread in gauss_widths:
        profile_sum = jnp.sum(jnp.exp(-tap_offsets * tap_offsets / (2.0 * spread * spread)))
        even_band = jnp.where(
            inside, jnp.exp(-offset * offset / (2.0 * spread * spread)) / profile_sum, 0.0
        )
        tables.append(even_band)
        tables.append(even_band * offset / spread)
    return jnp.stack(tables)


def match_kernel(coef_ref, pix_ref, mask_ref, tab_ref, right_ref, out_ref):
    step = pl.program_id(0)
    group, side_len, _ = pix_ref.shape
    bits = mask_ref[...]
    masked = jnp.where((bits & 7) == 0, pix_ref[...], jnp.zeros((), jnp.bfloat16))
    columns = jnp.dot(
        masked.reshape(group * side_len, side_len),
        right_ref[...],
        preferred_element_type=jnp.float32,
    ).astype(jnp.bfloat16)
    for g in range(group):
        base = (step * group + g) * 9
        rows = columns[g * side_len:(g + 1) * side_len]
        acc = jnp.zeros((side_len, side_len), jnp.float32)
        for m in range(3):
            even_band = tab_ref[2 * m]
            odd_band = tab_ref[2 * m + 1]
            left_a = (coef_ref[base + 3 * m] * even_band
                      + coef_ref[base + 3 * m + 1] * odd_band).astype(jnp.bfloat16)
            left_b = (coef_ref[base + 3 * m + 2] * even_band).astype(jnp.bfloat16)
            acc = acc + jnp.dot(
                left_a, rows[:, (2 * m) * side_len:(2 * m + 1) * side_len],
                preferred_element_type=jnp.float32,
            )
            acc = acc + jnp.dot(
                left_b, rows[:, (2 * m + 1) * side_len:(2 * m + 2) * side_len],
                preferred_element_type=jnp.float32,
            )
        out_ref[g] = acc.astype(jnp.bfloat16)


def match_blocks(pixels, mask_bits, coefficients, tables, right_bands):
    number, side_len, _ = pixels.shape
    steps = number // GROUP
    flops = number * 4 * side_len * side_len * 6 * side_len
    return pl.pallas_call(
        match_kernel,
        out_shape=jax.ShapeDtypeStruct(pixels.shape, jnp.bfloat16),
        grid=(steps,),
        in_specs=[
            pl.BlockSpec(memory_space=pltpu.SMEM),
            pl.BlockSpec((GROUP, side_len, side_len), lambda i: (i, 0, 0)),
            pl.BlockSpec((GROUP, side_len, side_len), lambda i: (i, 0, 0)),
            pl.BlockSpec(tables.shape, lambda i: (0, 0, 0)),
            pl.BlockSpec(right_bands.shape, lambda i: (0, 0)),
        ],
        out_specs=pl.BlockSpec((GROUP, side_len, side_len), lambda i: (i, 0, 0)),
        cost_estimate=pl.CostEstimate(
            flops=flops, transcendentals=0, bytes_accessed=number * side_len * side_len * 8
        ),
    )(coefficients.reshape(-1), pixels, mask_bits, tables, right_bands)


def shards(pixels, mask_bits, inv_var, owner, cell, coef_index, coef_table):
    blocks_here = pixels.shape[0]
    side_len = pixels.shape[1]
    patches = lax.axis_size("patch")
    visits = lax.axis_size("visit")
    devices = patches * visits
    segments = patches * CELLS
    rows_here = side_len // visits
    both = ("visit", "patch")
    tables = band_tables(side_len)
    right_bands = (
        jnp.transpose(tables, (2, 0, 1)).reshape(side_len, 6 * side_len).astype(jnp.bfloat16)
    )
    coefficients = coef_table[coef_index]
    matched_home = match_blocks(pixels, mask_bits, coefficients, tables, right_bands)
    by_row = jnp.transpose(matched_home, (1, 0, 2))
    weight = inv_var.astype(jnp.bfloat16)
    meta = jnp.concatenate([
        jnp.concatenate([weight, owner.astype(jnp.bfloat16)])[None, :],
        jnp.concatenate([cell.astype(jnp.bfloat16), jnp.zeros_like(weight)])[None, :],
        jnp.zeros((14, side_len), jnp.bfloat16),
    ])
    payload = jnp.concatenate(
        [by_row, jnp.broadcast_to(meta[None], (devices,) + meta.shape)], axis=1
    )
    received = lax.all_to_all(payload, both, split_axis=0, concat_axis=0, tiled=True)
    row_all = received[:, :blocks_here].reshape(devices * blocks_here, side_len)
    weight_all = received[:, blocks_here, :blocks_here].reshape(-1)
    owner_all = received[:, blocks_here, blocks_here:].reshape(-1).astype(jnp.int32)
    cell_all = received[:, blocks_here + 1, :blocks_here].reshape(-1).astype(jnp.int32)
    segment_all = owner_all * CELLS + cell_all
    picks = segment_all[None, :] == jnp.arange(segments, dtype=jnp.int32)[:, None]
    weighted = jnp.where(picks, weight_all[None, :], jnp.zeros((), jnp.bfloat16))
    numerator = jnp.dot(weighted, row_all, preferred_element_type=jnp.float32)
    owner_pick = (owner_all[None, :] == jnp.arange(patches, dtype=jnp.int32)[:, None]).astype(
        jnp.bfloat16
    )
    cell_pick = jnp.where(
        cell_all[None, :] == jnp.arange(CELLS, dtype=jnp.int32)[:, None],
        weight_all[None, :],
        jnp.zeros((), jnp.bfloat16),
    )
    weight_sum = lax.dot_general(
        owner_pick, cell_pick, (((1,), (1,)), ((), ())), preferred_element_type=jnp.float32
    ).reshape(segments)
    coadd_row = numerator / jnp.maximum(weight_sum, 1.0)[:, None]
    template_row = coadd_row.astype(jnp.bfloat16)
    block_pick = (
        segment_all[:, None] == jnp.arange(segments, dtype=jnp.int32)[None, :]
    ).astype(jnp.bfloat16)
    block_template = jnp.dot(block_pick, template_row, preferred_element_type=jnp.float32)
    difference_row = (row_all.astype(jnp.float32) - block_template).astype(jnp.bfloat16)
    returned = lax.all_to_all(
        difference_row.reshape(devices, blocks_here, side_len),
        both, split_axis=0, concat_axis=0, tiled=True,
    )
    difference = jnp.transpose(returned, (1, 0, 2))
    coadd_parts = lax.all_to_all(
        coadd_row.reshape(patches, CELLS, 1, side_len),
        "patch", split_axis=0, concat_axis=2, tiled=True,
    )
    coadd_part = coadd_parts.reshape(CELLS, rows_here, side_len)
    return (coadd_part, difference)


def solution(mesh):
    placed = (
        P(("visit", "patch"), None, None),
        P(("visit", "patch"), None, None),
        P(("visit", "patch")),
        P(("visit", "patch")),
        P(("visit", "patch")),
        P(("visit", "patch")),
        P(),
    )
    return jax.shard_map(
        shards,
        mesh=mesh,
        in_specs=placed,
        out_specs=(P("patch", "visit", None), P(("visit", "patch"), None, None)),
        check_vma=False,
    )
```

```python
import jax
import jax.numpy as jnp
import numpy as np
from jax import lax
from jax.experimental import pallas as pl
from jax.experimental.pallas import tpu as pltpu
from jax.sharding import PartitionSpec as P

CELLS = 64
KSIZE = 21
GROUP = 8


gauss_widths = (1.0, 2.0, 3.5)


def band_tables(side_len):
    tap_reach = KSIZE // 2
    position = np.arange(side_len).astype(np.float32)
    offset = position[:, None] - position[None, :]
    inside = np.abs(offset) <= tap_reach
    tap_offsets = np.arange(-tap_reach, tap_reach + 1).astype(np.float32)
    tables = []
    for spread in gauss_widths:
        spread = np.float32(spread)
        width = np.float32(2.0) * spread * spread
        profile_sum = np.sum(np.exp(-tap_offsets * tap_offsets / width), dtype=np.float32)
        even_band = np.where(inside, np.exp(-offset * offset / width) / profile_sum, 0.0)
        even_band = even_band.astype(np.float32)
        tables.append(even_band)
        tables.append((even_band * offset / spread).astype(np.float32))
    return np.stack(tables)


def match_kernel(coef_ref, pix_ref, mask_ref, tab_ref, right_ref, out_ref):
    step = pl.program_id(0)
    group, side_len, _ = pix_ref.shape
    bits = mask_ref[...]
    masked = jnp.where((bits & 7) == 0, pix_ref[...], jnp.zeros((), jnp.bfloat16))
    columns = jnp.dot(
        masked.reshape(group * side_len, side_len),
        right_ref[...],
        preferred_element_type=jnp.float32,
    ).astype(jnp.bfloat16)
    for g in range(group):
        base = (step * group + g) * 9
        rows = columns[g * side_len:(g + 1) * side_len]
        acc = jnp.zeros((side_len, side_len), jnp.float32)
        for m in range(3):
            even_band = tab_ref[2 * m]
            odd_band = tab_ref[2 * m + 1]
            left_a = (coef_ref[base + 3 * m] * even_band
                      + coef_ref[base + 3 * m + 1] * odd_band).astype(jnp.bfloat16)
            left_b = (coef_ref[base + 3 * m + 2] * even_band).astype(jnp.bfloat16)
            acc = acc + jnp.dot(
                left_a, rows[:, (2 * m) * side_len:(2 * m + 1) * side_len],
                preferred_element_type=jnp.float32,
            )
            acc = acc + jnp.dot(
                left_b, rows[:, (2 * m + 1) * side_len:(2 * m + 2) * side_len],
                preferred_element_type=jnp.float32,
            )
        out_ref[g] = acc.astype(jnp.bfloat16)


def match_blocks(pixels, mask_bits, coefficients, tables, right_bands):
    number, side_len, _ = pixels.shape
    steps = number // GROUP
    flops = number * 4 * side_len * side_len * 6 * side_len
    return pl.pallas_call(
        match_kernel,
        out_shape=jax.ShapeDtypeStruct(pixels.shape, jnp.bfloat16),
        grid=(steps,),
        in_specs=[
            pl.BlockSpec(memory_space=pltpu.SMEM),
            pl.BlockSpec((GROUP, side_len, side_len), lambda i: (i, 0, 0)),
            pl.BlockSpec((GROUP, side_len, side_len), lambda i: (i, 0, 0)),
            pl.BlockSpec(tables.shape, lambda i: (0, 0, 0)),
            pl.BlockSpec(right_bands.shape, lambda i: (0, 0)),
        ],
        out_specs=pl.BlockSpec((GROUP, side_len, side_len), lambda i: (i, 0, 0)),
        cost_estimate=pl.CostEstimate(
            flops=flops, transcendentals=0, bytes_accessed=number * side_len * side_len * 8
        ),
    )(coefficients.reshape(-1), pixels, mask_bits, tables, right_bands)


def shards(pixels, mask_bits, inv_var, owner, cell, coef_index, coef_table):
    blocks_here = pixels.shape[0]
    side_len = pixels.shape[1]
    patches = lax.axis_size("patch")
    visits = lax.axis_size("visit")
    devices = patches * visits
    segments = patches * CELLS
    rows_here = side_len // visits
    both = ("visit", "patch")
    tables = band_tables(side_len)
    right_bands = jnp.asarray(
        np.transpose(tables, (2, 0, 1)).reshape(side_len, 6 * side_len), jnp.bfloat16
    )
    tables = jnp.asarray(tables)
    coefficients = coef_table[coef_index]
    matched_home = match_blocks(pixels, mask_bits, coefficients, tables, right_bands)
    by_row = jnp.transpose(matched_home, (1, 0, 2))
    weight = inv_var.astype(jnp.bfloat16)
    meta = jnp.concatenate([
        jnp.concatenate([weight, owner.astype(jnp.bfloat16)])[None, :],
        jnp.concatenate([cell.astype(jnp.bfloat16), jnp.zeros_like(weight)])[None, :],
        jnp.zeros((14, side_len), jnp.bfloat16),
    ])
    payload = jnp.concatenate(
        [by_row, jnp.broadcast_to(meta[None], (devices,) + meta.shape)], axis=1
    )
    received = lax.all_to_all(payload, both, split_axis=0, concat_axis=0, tiled=True)
    row_all = received[:, :blocks_here].reshape(devices * blocks_here, side_len)
    weight_all = received[:, blocks_here, :blocks_here].reshape(-1)
    owner_all = received[:, blocks_here, blocks_here:].reshape(-1).astype(jnp.int32)
    cell_all = received[:, blocks_here + 1, :blocks_here].reshape(-1).astype(jnp.int32)
    segment_all = owner_all * CELLS + cell_all
    picks = segment_all[None, :] == jnp.arange(segments, dtype=jnp.int32)[:, None]
    weighted = jnp.where(picks, weight_all[None, :], jnp.zeros((), jnp.bfloat16))
    numerator = jnp.dot(weighted, row_all, preferred_element_type=jnp.float32)
    owner_pick = (owner_all[None, :] == jnp.arange(patches, dtype=jnp.int32)[:, None]).astype(
        jnp.bfloat16
    )
    cell_pick = jnp.where(
        cell_all[None, :] == jnp.arange(CELLS, dtype=jnp.int32)[:, None],
        weight_all[None, :],
        jnp.zeros((), jnp.bfloat16),
    )
    weight_sum = lax.dot_general(
        owner_pick, cell_pick, (((1,), (1,)), ((), ())), preferred_element_type=jnp.float32
    ).reshape(segments)
    coadd_row = numerator / jnp.maximum(weight_sum, 1.0)[:, None]
    template_row = coadd_row.astype(jnp.bfloat16)
    row_blocks = row_all.reshape(devices, blocks_here, side_len)
    segment_blocks = segment_all.reshape(devices, blocks_here)
    half = blocks_here // 2
    returned = []
    for part in range(2):
        part_rows = row_blocks[:, part * half:(part + 1) * half].reshape(-1, side_len)
        part_segments = segment_blocks[:, part * half:(part + 1) * half].reshape(-1)
        block_pick = (
            part_segments[:, None] == jnp.arange(segments, dtype=jnp.int32)[None, :]
        ).astype(jnp.bfloat16)
        block_template = jnp.dot(block_pick, template_row, preferred_element_type=jnp.float32)
        part_difference = (part_rows.astype(jnp.float32) - block_template).astype(jnp.bfloat16)
        returned.append(lax.all_to_all(
            part_difference.reshape(devices, half, side_len),
            both, split_axis=0, concat_axis=0, tiled=True,
        ))
    difference = jnp.transpose(jnp.concatenate(returned, axis=1), (1, 0, 2))
    coadd_parts = lax.all_to_all(
        coadd_row.reshape(patches, CELLS, 1, side_len),
        "patch", split_axis=0, concat_axis=2, tiled=True,
    )
    coadd_part = coadd_parts.reshape(CELLS, rows_here, side_len)
    return (coadd_part, difference)


def solution(mesh):
    placed = (
        P(("visit", "patch"), None, None),
        P(("visit", "patch"), None, None),
        P(("visit", "patch")),
        P(("visit", "patch")),
        P(("visit", "patch")),
        P(("visit", "patch")),
        P(),
    )
    return jax.shard_map(
        shards,
        mesh=mesh,
        in_specs=placed,
        out_specs=(P("patch", "visit", None), P(("visit", "patch"), None, None)),
        check_vma=False,
    )
```

```python
import jax
import jax.numpy as jnp
import numpy as np
from jax import lax
from jax.experimental import pallas as pl
from jax.experimental.pallas import tpu as pltpu
from jax.sharding import PartitionSpec as P

CELLS = 64
KSIZE = 21
GROUP = 8


gauss_widths = (1.0, 2.0, 3.5)


def band_tables(side_len):
    tap_reach = KSIZE // 2
    position = np.arange(side_len).astype(np.float32)
    offset = position[:, None] - position[None, :]
    inside = np.abs(offset) <= tap_reach
    tap_offsets = np.arange(-tap_reach, tap_reach + 1).astype(np.float32)
    tables = []
    for spread in gauss_widths:
        spread = np.float32(spread)
        width = np.float32(2.0) * spread * spread
        profile_sum = np.sum(np.exp(-tap_offsets * tap_offsets / width), dtype=np.float32)
        even_band = np.where(inside, np.exp(-offset * offset / width) / profile_sum, 0.0)
        even_band = even_band.astype(np.float32)
        tables.append(even_band)
        tables.append((even_band * offset / spread).astype(np.float32))
    return np.stack(tables)


def match_kernel(coef_ref, pix_ref, mask_ref, tab_ref, right_ref, out_ref):
    step = pl.program_id(0)
    group, side_len, _ = pix_ref.shape
    bits = mask_ref[...]
    masked = jnp.where((bits & 7) == 0, pix_ref[...], jnp.zeros((), jnp.bfloat16))
    columns = jnp.dot(
        masked.reshape(group * side_len, side_len),
        right_ref[...],
        preferred_element_type=jnp.float32,
    ).astype(jnp.bfloat16)
    for g in range(group):
        base = (step * group + g) * 9
        rows = columns[g * side_len:(g + 1) * side_len]
        acc = jnp.zeros((side_len, side_len), jnp.float32)
        for m in range(3):
            even_band = tab_ref[2 * m]
            odd_band = tab_ref[2 * m + 1]
            left_a = (coef_ref[base + 3 * m] * even_band
                      + coef_ref[base + 3 * m + 1] * odd_band).astype(jnp.bfloat16)
            left_b = (coef_ref[base + 3 * m + 2] * even_band).astype(jnp.bfloat16)
            acc = acc + jnp.dot(
                left_a, rows[:, (2 * m) * side_len:(2 * m + 1) * side_len],
                preferred_element_type=jnp.float32,
            )
            acc = acc + jnp.dot(
                left_b, rows[:, (2 * m + 1) * side_len:(2 * m + 2) * side_len],
                preferred_element_type=jnp.float32,
            )
        out_ref[g] = acc.astype(jnp.bfloat16)


def match_blocks(pixels, mask_bits, coefficients, tables, right_bands):
    number, side_len, _ = pixels.shape
    steps = number // GROUP
    flops = number * 4 * side_len * side_len * 6 * side_len
    return pl.pallas_call(
        match_kernel,
        out_shape=jax.ShapeDtypeStruct(pixels.shape, jnp.bfloat16),
        grid=(steps,),
        in_specs=[
            pl.BlockSpec(memory_space=pltpu.SMEM),
            pl.BlockSpec((GROUP, side_len, side_len), lambda i: (i, 0, 0)),
            pl.BlockSpec((GROUP, side_len, side_len), lambda i: (i, 0, 0)),
            pl.BlockSpec(tables.shape, lambda i: (0, 0, 0)),
            pl.BlockSpec(right_bands.shape, lambda i: (0, 0)),
        ],
        out_specs=pl.BlockSpec((GROUP, side_len, side_len), lambda i: (i, 0, 0)),
        cost_estimate=pl.CostEstimate(
            flops=flops, transcendentals=0, bytes_accessed=number * side_len * side_len * 8
        ),
    )(coefficients.reshape(-1), pixels, mask_bits, tables, right_bands)


def shards(pixels, mask_bits, inv_var, owner, cell, coef_index, coef_table):
    blocks_here = pixels.shape[0]
    side_len = pixels.shape[1]
    patches = lax.axis_size("patch")
    visits = lax.axis_size("visit")
    devices = patches * visits
    segments = patches * CELLS
    rows_here = side_len // visits
    both = ("visit", "patch")
    tables = band_tables(side_len)
    right_bands = jnp.asarray(
        np.transpose(tables, (2, 0, 1)).reshape(side_len, 6 * side_len), jnp.bfloat16
    )
    tables = jnp.asarray(tables)
    coefficients = coef_table[coef_index]
    matched_home = match_blocks(pixels, mask_bits, coefficients, tables, right_bands)
    by_row = jnp.transpose(matched_home, (1, 0, 2))
    weight = inv_var.astype(jnp.bfloat16)
    meta = jnp.concatenate([
        jnp.concatenate([weight, owner.astype(jnp.bfloat16)])[None, :],
        jnp.concatenate([cell.astype(jnp.bfloat16), jnp.zeros_like(weight)])[None, :],
        jnp.zeros((14, side_len), jnp.bfloat16),
    ])
    payload = jnp.concatenate(
        [by_row, jnp.broadcast_to(meta[None], (devices,) + meta.shape)], axis=1
    )
    received = lax.all_to_all(payload, both, split_axis=0, concat_axis=0, tiled=True)
    row_all = received[:, :blocks_here].reshape(devices * blocks_here, side_len)
    weight_all = received[:, blocks_here, :blocks_here].reshape(-1)
    owner_all = received[:, blocks_here, blocks_here:].reshape(-1).astype(jnp.int32)
    cell_all = received[:, blocks_here + 1, :blocks_here].reshape(-1).astype(jnp.int32)
    segment_all = owner_all * CELLS + cell_all
    picks = segment_all[None, :] == jnp.arange(segments, dtype=jnp.int32)[:, None]
    weighted = jnp.where(picks, weight_all[None, :], jnp.zeros((), jnp.bfloat16))
    numerator = jnp.dot(weighted, row_all, preferred_element_type=jnp.float32)
    owner_pick = (owner_all[None, :] == jnp.arange(patches, dtype=jnp.int32)[:, None]).astype(
        jnp.bfloat16
    )
    cell_pick = jnp.where(
        cell_all[None, :] == jnp.arange(CELLS, dtype=jnp.int32)[:, None],
        weight_all[None, :],
        jnp.zeros((), jnp.bfloat16),
    )
    weight_sum = lax.dot_general(
        owner_pick, cell_pick, (((1,), (1,)), ((), ())), preferred_element_type=jnp.float32
    ).reshape(segments)
    coadd_row = numerator / jnp.maximum(weight_sum, 1.0)[:, None]
    template_row = coadd_row.astype(jnp.bfloat16)
    block_pick = (
        segment_all[:, None] == jnp.arange(segments, dtype=jnp.int32)[None, :]
    ).astype(jnp.bfloat16)
    block_template = jnp.dot(block_pick, template_row, preferred_element_type=jnp.float32)
    difference_row = (row_all.astype(jnp.float32) - block_template).astype(jnp.bfloat16)
    returned = lax.all_to_all(
        difference_row.reshape(devices, blocks_here, side_len),
        both, split_axis=0, concat_axis=0, tiled=True,
    )
    difference = jnp.transpose(returned, (1, 0, 2))
    coadd_parts = lax.all_to_all(
        coadd_row.reshape(patches, CELLS, 1, side_len),
        "patch", split_axis=0, concat_axis=2, tiled=True,
    )
    coadd_part = coadd_parts.reshape(CELLS, rows_here, side_len)
    return (coadd_part, difference)


def solution(mesh):
    placed = (
        P(("visit", "patch"), None, None),
        P(("visit", "patch"), None, None),
        P(("visit", "patch")),
        P(("visit", "patch")),
        P(("visit", "patch")),
        P(("visit", "patch")),
        P(),
    )
    return jax.shard_map(
        shards,
        mesh=mesh,
        in_specs=placed,
        out_specs=(P("patch", "visit", None), P(("visit", "patch"), None, None)),
        check_vma=False,
    )
```

```python
import jax
import jax.numpy as jnp
import numpy as np
from jax import lax
from jax.experimental import pallas as pl
from jax.experimental.pallas import tpu as pltpu
from jax.sharding import PartitionSpec as P

CELLS = 64
KSIZE = 21
GROUP = 8


gauss_widths = (1.0, 2.0, 3.5)


def band_tables(side_len):
    tap_reach = KSIZE // 2
    position = np.arange(side_len).astype(np.float32)
    offset = position[:, None] - position[None, :]
    inside = np.abs(offset) <= tap_reach
    tap_offsets = np.arange(-tap_reach, tap_reach + 1).astype(np.float32)
    tables = []
    for spread in gauss_widths:
        spread = np.float32(spread)
        width = np.float32(2.0) * spread * spread
        profile_sum = np.sum(np.exp(-tap_offsets * tap_offsets / width), dtype=np.float32)
        even_band = np.where(inside, np.exp(-offset * offset / width) / profile_sum, 0.0)
        even_band = even_band.astype(np.float32)
        tables.append(even_band)
        tables.append((even_band * offset / spread).astype(np.float32))
    return np.stack(tables)


def match_kernel(coef_ref, pix_ref, mask_ref, tab_ref, right_ref, out_ref):
    step = pl.program_id(0)
    group, side_len, _ = pix_ref.shape
    bits = mask_ref[...]
    masked = jnp.where((bits & 7) == 0, pix_ref[...], jnp.zeros((), jnp.bfloat16))
    columns = jnp.dot(
        masked.reshape(group * side_len, side_len),
        right_ref[...],
        preferred_element_type=jnp.float32,
    ).astype(jnp.bfloat16)
    for g in range(group):
        base = (step * group + g) * 9
        rows = columns[g * side_len:(g + 1) * side_len]
        acc = jnp.zeros((side_len, side_len), jnp.float32)
        for m in range(3):
            even_band = tab_ref[2 * m]
            odd_band = tab_ref[2 * m + 1]
            left_a = (coef_ref[base + 3 * m] * even_band
                      + coef_ref[base + 3 * m + 1] * odd_band).astype(jnp.bfloat16)
            left_b = (coef_ref[base + 3 * m + 2] * even_band).astype(jnp.bfloat16)
            acc = acc + jnp.dot(
                left_a, rows[:, (2 * m) * side_len:(2 * m + 1) * side_len],
                preferred_element_type=jnp.float32,
            )
            acc = acc + jnp.dot(
                left_b, rows[:, (2 * m + 1) * side_len:(2 * m + 2) * side_len],
                preferred_element_type=jnp.float32,
            )
        out_ref[g] = acc.astype(jnp.bfloat16)


def match_blocks(pixels, mask_bits, coefficients, tables, right_bands):
    number, side_len, _ = pixels.shape
    steps = number // GROUP
    flops = number * 4 * side_len * side_len * 6 * side_len
    return pl.pallas_call(
        match_kernel,
        out_shape=jax.ShapeDtypeStruct(pixels.shape, jnp.bfloat16),
        grid=(steps,),
        in_specs=[
            pl.BlockSpec(memory_space=pltpu.SMEM),
            pl.BlockSpec((GROUP, side_len, side_len), lambda i: (i, 0, 0)),
            pl.BlockSpec((GROUP, side_len, side_len), lambda i: (i, 0, 0)),
            pl.BlockSpec(tables.shape, lambda i: (0, 0, 0)),
            pl.BlockSpec(right_bands.shape, lambda i: (0, 0)),
        ],
        out_specs=pl.BlockSpec((GROUP, side_len, side_len), lambda i: (i, 0, 0)),
        cost_estimate=pl.CostEstimate(
            flops=flops, transcendentals=0, bytes_accessed=number * side_len * side_len * 8
        ),
    )(coefficients.reshape(-1), pixels, mask_bits, tables, right_bands)


def shards(pixels, mask_bits, inv_var, owner, cell, coef_index, coef_table):
    blocks_here = pixels.shape[0]
    side_len = pixels.shape[1]
    patches = lax.axis_size("patch")
    visits = lax.axis_size("visit")
    devices = patches * visits
    segments = patches * CELLS
    rows_here = side_len // visits
    both = ("visit", "patch")
    tables = band_tables(side_len)
    right_bands = jnp.asarray(
        np.transpose(tables, (2, 0, 1)).reshape(side_len, 6 * side_len), jnp.bfloat16
    )
    tables = jnp.asarray(tables)
    coefficients = coef_table[coef_index]
    matched_home = match_blocks(pixels, mask_bits, coefficients, tables, right_bands)
    weight = inv_var.astype(jnp.bfloat16)
    meta = jnp.concatenate([
        jnp.concatenate([weight, owner.astype(jnp.bfloat16)])[None, :],
        jnp.concatenate([cell.astype(jnp.bfloat16), jnp.zeros_like(weight)])[None, :],
        jnp.zeros((14, side_len), jnp.bfloat16),
    ])
    by_row = jnp.transpose(matched_home, (1, 0, 2))
    meta_all = lax.all_to_all(
        jnp.broadcast_to(meta[None], (devices,) + meta.shape), both,
        split_axis=0, concat_axis=0, tiled=True,
    )
    row_all = lax.all_to_all(by_row, both, split_axis=0, concat_axis=0, tiled=True)
    row_all = row_all.reshape(devices * blocks_here, side_len)
    weight_all = meta_all[:, 0, :blocks_here].reshape(-1)
    owner_all = meta_all[:, 0, blocks_here:].reshape(-1).astype(jnp.int32)
    cell_all = meta_all[:, 1, :blocks_here].reshape(-1).astype(jnp.int32)
    segment_all = owner_all * CELLS + cell_all
    picks = segment_all[None, :] == jnp.arange(segments, dtype=jnp.int32)[:, None]
    weighted = jnp.where(picks, weight_all[None, :], jnp.zeros((), jnp.bfloat16))
    numerator = jnp.dot(weighted, row_all, preferred_element_type=jnp.float32)
    owner_pick = (owner_all[None, :] == jnp.arange(patches, dtype=jnp.int32)[:, None]).astype(
        jnp.bfloat16
    )
    cell_pick = jnp.where(
        cell_all[None, :] == jnp.arange(CELLS, dtype=jnp.int32)[:, None],
        weight_all[None, :],
        jnp.zeros((), jnp.bfloat16),
    )
    weight_sum = lax.dot_general(
        owner_pick, cell_pick, (((1,), (1,)), ((), ())), preferred_element_type=jnp.float32
    ).reshape(segments)
    coadd_row = numerator / jnp.maximum(weight_sum, 1.0)[:, None]
    template_row = coadd_row.astype(jnp.bfloat16)
    block_pick = (
        segment_all[:, None] == jnp.arange(segments, dtype=jnp.int32)[None, :]
    ).astype(jnp.bfloat16)
    block_template = jnp.dot(block_pick, template_row, preferred_element_type=jnp.float32)
    difference_row = (row_all.astype(jnp.float32) - block_template).astype(jnp.bfloat16)
    returned = lax.all_to_all(
        difference_row.reshape(devices, blocks_here, side_len),
        both, split_axis=0, concat_axis=0, tiled=True,
    )
    difference = jnp.transpose(returned, (1, 0, 2))
    coadd_parts = lax.all_to_all(
        coadd_row.reshape(patches, CELLS, 1, side_len),
        "patch", split_axis=0, concat_axis=2, tiled=True,
    )
    coadd_part = coadd_parts.reshape(CELLS, rows_here, side_len)
    return (coadd_part, difference)


def solution(mesh):
    placed = (
        P(("visit", "patch"), None, None),
        P(("visit", "patch"), None, None),
        P(("visit", "patch")),
        P(("visit", "patch")),
        P(("visit", "patch")),
        P(("visit", "patch")),
        P(),
    )
    return jax.shard_map(
        shards,
        mesh=mesh,
        in_specs=placed,
        out_specs=(P("patch", "visit", None), P(("visit", "patch"), None, None)),
        check_vma=False,
    )
```

```python
import jax
import jax.numpy as jnp
import numpy as np
from jax import lax
from jax.experimental import pallas as pl
from jax.experimental.pallas import tpu as pltpu
from jax.sharding import PartitionSpec as P

CELLS = 64
KSIZE = 21
GROUP = 8


gauss_widths = (1.0, 2.0, 3.5)


def band_tables(side_len):
    tap_reach = KSIZE // 2
    position = np.arange(side_len).astype(np.float32)
    offset = position[:, None] - position[None, :]
    inside = np.abs(offset) <= tap_reach
    tap_offsets = np.arange(-tap_reach, tap_reach + 1).astype(np.float32)
    tables = []
    for spread in gauss_widths:
        spread = np.float32(spread)
        width = np.float32(2.0) * spread * spread
        profile_sum = np.sum(np.exp(-tap_offsets * tap_offsets / width), dtype=np.float32)
        even_band = np.where(inside, np.exp(-offset * offset / width) / profile_sum, 0.0)
        even_band = even_band.astype(np.float32)
        tables.append(even_band)
        tables.append((even_band * offset / spread).astype(np.float32))
    return np.stack(tables)


def match_kernel(coef_ref, pix_ref, mask_ref, tab_ref, right_ref, out_ref):
    step = pl.program_id(0)
    group, side_len, _ = pix_ref.shape
    bits = mask_ref[...]
    masked = jnp.where((bits & 7) == 0, pix_ref[...], jnp.zeros((), jnp.bfloat16))
    columns = jnp.dot(
        masked.reshape(group * side_len, side_len),
        right_ref[...],
        preferred_element_type=jnp.float32,
    ).astype(jnp.bfloat16)
    for g in range(group):
        base = (step * group + g) * 9
        rows = columns[g * side_len:(g + 1) * side_len]
        stacked = jnp.concatenate(
            [rows[:, s * side_len:(s + 1) * side_len] for s in range(6)], axis=0
        )
        lefts = []
        for m in range(3):
            even_band = tab_ref[2 * m]
            odd_band = tab_ref[2 * m + 1]
            lefts.append((coef_ref[base + 3 * m] * even_band
                          + coef_ref[base + 3 * m + 1] * odd_band).astype(jnp.bfloat16))
            lefts.append((coef_ref[base + 3 * m + 2] * even_band).astype(jnp.bfloat16))
        left = jnp.concatenate(lefts, axis=1)
        out_ref[g] = jnp.dot(left, stacked, preferred_element_type=jnp.float32).astype(
            jnp.bfloat16
        )


def match_blocks(pixels, mask_bits, coefficients, tables, right_bands):
    number, side_len, _ = pixels.shape
    steps = number // GROUP
    flops = number * 4 * side_len * side_len * 6 * side_len
    return pl.pallas_call(
        match_kernel,
        out_shape=jax.ShapeDtypeStruct(pixels.shape, jnp.bfloat16),
        grid=(steps,),
        in_specs=[
            pl.BlockSpec(memory_space=pltpu.SMEM),
            pl.BlockSpec((GROUP, side_len, side_len), lambda i: (i, 0, 0)),
            pl.BlockSpec((GROUP, side_len, side_len), lambda i: (i, 0, 0)),
            pl.BlockSpec(tables.shape, lambda i: (0, 0, 0)),
            pl.BlockSpec(right_bands.shape, lambda i: (0, 0)),
        ],
        out_specs=pl.BlockSpec((GROUP, side_len, side_len), lambda i: (i, 0, 0)),
        cost_estimate=pl.CostEstimate(
            flops=flops, transcendentals=0, bytes_accessed=number * side_len * side_len * 8
        ),
    )(coefficients.reshape(-1), pixels, mask_bits, tables, right_bands)


def shards(pixels, mask_bits, inv_var, owner, cell, coef_index, coef_table):
    blocks_here = pixels.shape[0]
    side_len = pixels.shape[1]
    patches = lax.axis_size("patch")
    visits = lax.axis_size("visit")
    devices = patches * visits
    segments = patches * CELLS
    rows_here = side_len // visits
    both = ("visit", "patch")
    tables = band_tables(side_len)
    right_bands = jnp.asarray(
        np.transpose(tables, (2, 0, 1)).reshape(side_len, 6 * side_len), jnp.bfloat16
    )
    tables = jnp.asarray(tables)
    coefficients = coef_table[coef_index]
    matched_home = match_blocks(pixels, mask_bits, coefficients, tables, right_bands)
    by_row = jnp.transpose(matched_home, (1, 0, 2))
    weight = inv_var.astype(jnp.bfloat16)
    meta = jnp.concatenate([
        jnp.concatenate([weight, owner.astype(jnp.bfloat16)])[None, :],
        jnp.concatenate([cell.astype(jnp.bfloat16), jnp.zeros_like(weight)])[None, :],
        jnp.zeros((14, side_len), jnp.bfloat16),
    ])
    payload = jnp.concatenate(
        [by_row, jnp.broadcast_to(meta[None], (devices,) + meta.shape)], axis=1
    )
    received = lax.all_to_all(payload, both, split_axis=0, concat_axis=0, tiled=True)
    row_all = received[:, :blocks_here].reshape(devices * blocks_here, side_len)
    weight_all = received[:, blocks_here, :blocks_here].reshape(-1)
    owner_all = received[:, blocks_here, blocks_here:].reshape(-1).astype(jnp.int32)
    cell_all = received[:, blocks_here + 1, :blocks_here].reshape(-1).astype(jnp.int32)
    segment_all = owner_all * CELLS + cell_all
    picks = segment_all[None, :] == jnp.arange(segments, dtype=jnp.int32)[:, None]
    weighted = jnp.where(picks, weight_all[None, :], jnp.zeros((), jnp.bfloat16))
    numerator = jnp.dot(weighted, row_all, preferred_element_type=jnp.float32)
    owner_pick = (owner_all[None, :] == jnp.arange(patches, dtype=jnp.int32)[:, None]).astype(
        jnp.bfloat16
    )
    cell_pick = jnp.where(
        cell_all[None, :] == jnp.arange(CELLS, dtype=jnp.int32)[:, None],
        weight_all[None, :],
        jnp.zeros((), jnp.bfloat16),
    )
    weight_sum = lax.dot_general(
        owner_pick, cell_pick, (((1,), (1,)), ((), ())), preferred_element_type=jnp.float32
    ).reshape(segments)
    coadd_row = numerator / jnp.maximum(weight_sum, 1.0)[:, None]
    template_row = coadd_row.astype(jnp.bfloat16)
    block_pick = (
        segment_all[:, None] == jnp.arange(segments, dtype=jnp.int32)[None, :]
    ).astype(jnp.bfloat16)
    block_template = jnp.dot(block_pick, template_row, preferred_element_type=jnp.float32)
    difference_row = (row_all.astype(jnp.float32) - block_template).astype(jnp.bfloat16)
    returned = lax.all_to_all(
        difference_row.reshape(devices, blocks_here, side_len),
        both, split_axis=0, concat_axis=0, tiled=True,
    )
    difference = jnp.transpose(returned, (1, 0, 2))
    coadd_parts = lax.all_to_all(
        coadd_row.reshape(patches, CELLS, 1, side_len),
        "patch", split_axis=0, concat_axis=2, tiled=True,
    )
    coadd_part = coadd_parts.reshape(CELLS, rows_here, side_len)
    return (coadd_part, difference)


def solution(mesh):
    placed = (
        P(("visit", "patch"), None, None),
        P(("visit", "patch"), None, None),
        P(("visit", "patch")),
        P(("visit", "patch")),
        P(("visit", "patch")),
        P(("visit", "patch")),
        P(),
    )
    return jax.shard_map(
        shards,
        mesh=mesh,
        in_specs=placed,
        out_specs=(P("patch", "visit", None), P(("visit", "patch"), None, None)),
        check_vma=False,
    )
```

```python
import jax
import jax.numpy as jnp
import numpy as np
from jax import lax
from jax.experimental import pallas as pl
from jax.experimental.pallas import tpu as pltpu
from jax.sharding import PartitionSpec as P

CELLS = 64
KSIZE = 21
GROUP = 8


gauss_widths = (1.0, 2.0, 3.5)


def band_tables(side_len):
    tap_reach = KSIZE // 2
    position = np.arange(side_len).astype(np.float32)
    offset = position[:, None] - position[None, :]
    inside = np.abs(offset) <= tap_reach
    tap_offsets = np.arange(-tap_reach, tap_reach + 1).astype(np.float32)
    tables = []
    for spread in gauss_widths:
        spread = np.float32(spread)
        width = np.float32(2.0) * spread * spread
        profile_sum = np.sum(np.exp(-tap_offsets * tap_offsets / width), dtype=np.float32)
        even_band = np.where(inside, np.exp(-offset * offset / width) / profile_sum, 0.0)
        even_band = even_band.astype(np.float32)
        tables.append(even_band)
        tables.append((even_band * offset / spread).astype(np.float32))
    return np.stack(tables)


def match_kernel(index_ref, coef_ref, pix_ref, mask_ref, tab_ref, right_ref, out_ref):
    step = pl.program_id(0)
    group, side_len, _ = pix_ref.shape
    bits = mask_ref[...]
    masked = jnp.where((bits & 7) == 0, pix_ref[...], jnp.zeros((), jnp.bfloat16))
    columns = jnp.dot(
        masked.reshape(group * side_len, side_len),
        right_ref[...],
        preferred_element_type=jnp.float32,
    ).astype(jnp.bfloat16)
    for g in range(group):
        chosen = jnp.minimum(jnp.maximum(index_ref[step * group + g], 0), coef_ref.shape[0] // 9 - 1)
        base = chosen * 9
        rows = columns[g * side_len:(g + 1) * side_len]
        acc = jnp.zeros((side_len, side_len), jnp.float32)
        for m in range(3):
            even_band = tab_ref[2 * m]
            odd_band = tab_ref[2 * m + 1]
            left_a = (coef_ref[base + 3 * m] * even_band
                      + coef_ref[base + 3 * m + 1] * odd_band).astype(jnp.bfloat16)
            left_b = (coef_ref[base + 3 * m + 2] * even_band).astype(jnp.bfloat16)
            acc = acc + jnp.dot(
                left_a, rows[:, (2 * m) * side_len:(2 * m + 1) * side_len],
                preferred_element_type=jnp.float32,
            )
            acc = acc + jnp.dot(
                left_b, rows[:, (2 * m + 1) * side_len:(2 * m + 2) * side_len],
                preferred_element_type=jnp.float32,
            )
        out_ref[g] = acc.astype(jnp.bfloat16)


def match_blocks(pixels, mask_bits, coef_index, coef_table, tables, right_bands):
    number, side_len, _ = pixels.shape
    steps = number // GROUP
    flops = number * 4 * side_len * side_len * 6 * side_len
    return pl.pallas_call(
        match_kernel,
        out_shape=jax.ShapeDtypeStruct(pixels.shape, jnp.bfloat16),
        grid=(steps,),
        in_specs=[
            pl.BlockSpec(memory_space=pltpu.SMEM),
            pl.BlockSpec(memory_space=pltpu.SMEM),
            pl.BlockSpec((GROUP, side_len, side_len), lambda i: (i, 0, 0)),
            pl.BlockSpec((GROUP, side_len, side_len), lambda i: (i, 0, 0)),
            pl.BlockSpec(tables.shape, lambda i: (0, 0, 0)),
            pl.BlockSpec(right_bands.shape, lambda i: (0, 0)),
        ],
        out_specs=pl.BlockSpec((GROUP, side_len, side_len), lambda i: (i, 0, 0)),
        cost_estimate=pl.CostEstimate(
            flops=flops, transcendentals=0, bytes_accessed=number * side_len * side_len * 8
        ),
    )(coef_index, coef_table.reshape(-1), pixels, mask_bits, tables, right_bands)


def shards(pixels, mask_bits, inv_var, owner, cell, coef_index, coef_table):
    blocks_here = pixels.shape[0]
    side_len = pixels.shape[1]
    patches = lax.axis_size("patch")
    visits = lax.axis_size("visit")
    devices = patches * visits
    segments = patches * CELLS
    rows_here = side_len // visits
    both = ("visit", "patch")
    tables = band_tables(side_len)
    right_bands = jnp.asarray(
        np.transpose(tables, (2, 0, 1)).reshape(side_len, 6 * side_len), jnp.bfloat16
    )
    tables = jnp.asarray(tables)
    matched_home = match_blocks(pixels, mask_bits, coef_index, coef_table, tables, right_bands)
    meta = jnp.stack([
        inv_var,
        owner.astype(jnp.float32),
        cell.astype(jnp.float32),
        jnp.zeros_like(inv_var),
    ]).astype(jnp.bfloat16).reshape(2, 2 * blocks_here)
    meta = jnp.pad(meta, ((0, 14), (0, side_len - 2 * blocks_here)))
    meta_blocks = jnp.broadcast_to(meta[:, None, :], (16, side_len, side_len))
    payload = jnp.transpose(jnp.concatenate([matched_home, meta_blocks], axis=0), (1, 0, 2))
    received = lax.all_to_all(payload, both, split_axis=0, concat_axis=0, tiled=True)
    row_all = received[:, :blocks_here].reshape(devices * blocks_here, side_len)
    weight_all = received[:, blocks_here, :blocks_here].reshape(-1)
    owner_all = received[:, blocks_here, blocks_here:].reshape(-1).astype(jnp.int32)
    cell_all = received[:, blocks_here + 1, :blocks_here].reshape(-1).astype(jnp.int32)
    segment_all = owner_all * CELLS + cell_all
    picks = segment_all[None, :] == jnp.arange(segments, dtype=jnp.int32)[:, None]
    weighted = jnp.where(picks, weight_all[None, :], jnp.zeros((), jnp.bfloat16))
    numerator = jnp.dot(weighted, row_all, preferred_element_type=jnp.float32)
    owner_pick = (owner_all[None, :] == jnp.arange(patches, dtype=jnp.int32)[:, None]).astype(
        jnp.bfloat16
    )
    cell_pick = jnp.where(
        cell_all[None, :] == jnp.arange(CELLS, dtype=jnp.int32)[:, None],
        weight_all[None, :],
        jnp.zeros((), jnp.bfloat16),
    )
    weight_sum = lax.dot_general(
        owner_pick, cell_pick, (((1,), (1,)), ((), ())), preferred_element_type=jnp.float32
    ).reshape(segments)
    coadd_row = numerator / jnp.maximum(weight_sum, 1.0)[:, None]
    template_row = coadd_row.astype(jnp.bfloat16)
    block_pick = (
        segment_all[:, None] == jnp.arange(segments, dtype=jnp.int32)[None, :]
    ).astype(jnp.bfloat16)
    block_template = jnp.dot(block_pick, template_row, preferred_element_type=jnp.float32)
    difference_row = (row_all.astype(jnp.float32) - block_template).astype(jnp.bfloat16)
    returned = lax.all_to_all(
        difference_row.reshape(devices, blocks_here, side_len),
        both, split_axis=0, concat_axis=0, tiled=True,
    )
    difference = jnp.transpose(returned, (1, 0, 2))
    coadd_parts = lax.all_to_all(
        coadd_row.reshape(patches, CELLS, 1, side_len),
        "patch", split_axis=0, concat_axis=2, tiled=True,
    )
    coadd_part = coadd_parts.reshape(CELLS, rows_here, side_len)
    return (coadd_part, difference)


def solution(mesh):
    placed = (
        P(("visit", "patch"), None, None),
        P(("visit", "patch"), None, None),
        P(("visit", "patch")),
        P(("visit", "patch")),
        P(("visit", "patch")),
        P(("visit", "patch")),
        P(),
    )
    return jax.shard_map(
        shards,
        mesh=mesh,
        in_specs=placed,
        out_specs=(P("patch", "visit", None), P(("visit", "patch"), None, None)),
        check_vma=False,
    )
```

```python
import jax
import jax.numpy as jnp
import numpy as np
from jax import lax
from jax.experimental import pallas as pl
from jax.experimental.pallas import tpu as pltpu
from jax.sharding import PartitionSpec as P

CELLS = 64
KSIZE = 21
GROUP = 8


gauss_widths = (1.0, 2.0, 3.5)


def band_tables(side_len):
    tap_reach = KSIZE // 2
    position = np.arange(side_len).astype(np.float32)
    offset = position[:, None] - position[None, :]
    inside = np.abs(offset) <= tap_reach
    tap_offsets = np.arange(-tap_reach, tap_reach + 1).astype(np.float32)
    tables = []
    for spread in gauss_widths:
        spread = np.float32(spread)
        width = np.float32(2.0) * spread * spread
        profile_sum = np.sum(np.exp(-tap_offsets * tap_offsets / width), dtype=np.float32)
        even_band = np.where(inside, np.exp(-offset * offset / width) / profile_sum, 0.0)
        even_band = even_band.astype(np.float32)
        tables.append(even_band)
        tables.append((even_band * offset / spread).astype(np.float32))
    return np.stack(tables)


def match_kernel(index_ref, coef_ref, pix_ref, mask_ref, tab_ref, right_ref, meta_ref, out_ref):
    step = pl.program_id(0)
    group, side_len, _ = pix_ref.shape
    blocks = index_ref.shape[0]

    @pl.when(step * group < blocks)
    def _():
        bits = mask_ref[...]
        masked = jnp.where((bits & 7) == 0, pix_ref[...], jnp.zeros((), jnp.bfloat16))
        columns = jnp.dot(
            masked.reshape(group * side_len, side_len),
            right_ref[...],
            preferred_element_type=jnp.float32,
        ).astype(jnp.bfloat16)
        for g in range(group):
            chosen = jnp.minimum(
                jnp.maximum(index_ref[step * group + g], 0), coef_ref.shape[0] - 1
            )
            rows = columns[g * side_len:(g + 1) * side_len]
            acc = jnp.zeros((side_len, side_len), jnp.float32)
            for m in range(3):
                even_band = tab_ref[2 * m]
                odd_band = tab_ref[2 * m + 1]
                left_a = (coef_ref[chosen, 3 * m] * even_band
                          + coef_ref[chosen, 3 * m + 1] * odd_band).astype(jnp.bfloat16)
                left_b = (coef_ref[chosen, 3 * m + 2] * even_band).astype(jnp.bfloat16)
                acc = acc + jnp.dot(
                    left_a, rows[:, (2 * m) * side_len:(2 * m + 1) * side_len],
                    preferred_element_type=jnp.float32,
                )
                acc = acc + jnp.dot(
                    left_b, rows[:, (2 * m + 1) * side_len:(2 * m + 2) * side_len],
                    preferred_element_type=jnp.float32,
                )
            out_ref[g] = acc.astype(jnp.bfloat16)

    @pl.when(step * group >= blocks)
    def _():
        for g in range(group):
            line = meta_ref[g:g + 1, :].astype(jnp.bfloat16)
            out_ref[g] = jnp.broadcast_to(line, (side_len, side_len))


def match_blocks(pixels, mask_bits, coef_index, coef_table, tables, right_bands, meta):
    number, side_len, _ = pixels.shape
    steps = number // GROUP
    extra = meta.shape[0] // GROUP
    flops = number * 4 * side_len * side_len * 6 * side_len

    def block_at(i):
        return (jnp.minimum(i, steps - 1), 0, 0)

    return pl.pallas_call(
        match_kernel,
        out_shape=jax.ShapeDtypeStruct((number + meta.shape[0], side_len, side_len), jnp.bfloat16),
        grid=(steps + extra,),
        in_specs=[
            pl.BlockSpec(memory_space=pltpu.SMEM),
            pl.BlockSpec(memory_space=pltpu.SMEM),
            pl.BlockSpec((GROUP, side_len, side_len), block_at),
            pl.BlockSpec((GROUP, side_len, side_len), block_at),
            pl.BlockSpec(tables.shape, lambda i: (0, 0, 0)),
            pl.BlockSpec(right_bands.shape, lambda i: (0, 0)),
            pl.BlockSpec((GROUP, side_len), lambda i: (jnp.maximum(i - steps, 0), 0)),
        ],
        out_specs=pl.BlockSpec((GROUP, side_len, side_len), lambda i: (i, 0, 0)),
        cost_estimate=pl.CostEstimate(
            flops=flops, transcendentals=0, bytes_accessed=number * side_len * side_len * 8
        ),
    )(coef_index, coef_table, pixels, mask_bits, tables, right_bands, meta)


def shards(pixels, mask_bits, inv_var, owner, cell, coef_index, coef_table):
    blocks_here = pixels.shape[0]
    side_len = pixels.shape[1]
    patches = lax.axis_size("patch")
    visits = lax.axis_size("visit")
    devices = patches * visits
    segments = patches * CELLS
    rows_here = side_len // visits
    both = ("visit", "patch")
    tables = band_tables(side_len)
    right_bands = jnp.asarray(
        np.transpose(tables, (2, 0, 1)).reshape(side_len, 6 * side_len), jnp.bfloat16
    )
    tables = jnp.asarray(tables)
    meta = jnp.stack([
        inv_var.astype(jnp.bfloat16).astype(jnp.float32),
        owner.astype(jnp.float32),
        cell.astype(jnp.float32),
        jnp.zeros_like(inv_var),
    ]).reshape(2, 2 * blocks_here)
    meta = jnp.pad(meta, ((0, 14), (0, side_len - 2 * blocks_here)))
    matched_home = match_blocks(
        pixels, mask_bits, coef_index, coef_table, tables, right_bands, meta
    )
    payload = jnp.transpose(matched_home, (1, 0, 2))
    received = lax.all_to_all(payload, both, split_axis=0, concat_axis=0, tiled=True)
    row_all = received[:, :blocks_here].reshape(devices * blocks_here, side_len)
    weight_all = received[:, blocks_here, :blocks_here].reshape(-1)
    owner_all = received[:, blocks_here, blocks_here:].reshape(-1).astype(jnp.int32)
    cell_all = received[:, blocks_here + 1, :blocks_here].reshape(-1).astype(jnp.int32)
    segment_all = owner_all * CELLS + cell_all
    picks = segment_all[None, :] == jnp.arange(segments, dtype=jnp.int32)[:, None]
    weighted = jnp.where(picks, weight_all[None, :], jnp.zeros((), jnp.bfloat16))
    numerator = jnp.dot(weighted, row_all, preferred_element_type=jnp.float32)
    owner_pick = (owner_all[None, :] == jnp.arange(patches, dtype=jnp.int32)[:, None]).astype(
        jnp.bfloat16
    )
    cell_pick = jnp.where(
        cell_all[None, :] == jnp.arange(CELLS, dtype=jnp.int32)[:, None],
        weight_all[None, :],
        jnp.zeros((), jnp.bfloat16),
    )
    weight_sum = lax.dot_general(
        owner_pick, cell_pick, (((1,), (1,)), ((), ())), preferred_element_type=jnp.float32
    ).reshape(segments)
    coadd_row = numerator / jnp.maximum(weight_sum, 1.0)[:, None]
    template_row = coadd_row.astype(jnp.bfloat16)
    block_pick = (
        segment_all[:, None] == jnp.arange(segments, dtype=jnp.int32)[None, :]
    ).astype(jnp.bfloat16)
    block_template = jnp.dot(block_pick, template_row, preferred_element_type=jnp.float32)
    difference_row = (row_all.astype(jnp.float32) - block_template).astype(jnp.bfloat16)
    returned = lax.all_to_all(
        difference_row.reshape(devices, blocks_here, side_len),
        both, split_axis=0, concat_axis=0, tiled=True,
    )
    difference = jnp.transpose(returned, (1, 0, 2))
    coadd_parts = lax.all_to_all(
        coadd_row.reshape(patches, CELLS, 1, side_len),
        "patch", split_axis=0, concat_axis=2, tiled=True,
    )
    coadd_part = coadd_parts.reshape(CELLS, rows_here, side_len)
    return (coadd_part, difference)


def solution(mesh):
    placed = (
        P(("visit", "patch"), None, None),
        P(("visit", "patch"), None, None),
        P(("visit", "patch")),
        P(("visit", "patch")),
        P(("visit", "patch")),
        P(("visit", "patch")),
        P(),
    )
    return jax.shard_map(
        shards,
        mesh=mesh,
        in_specs=placed,
        out_specs=(P("patch", "visit", None), P(("visit", "patch"), None, None)),
        check_vma=False,
    )
```

```python
import jax
import jax.numpy as jnp
import numpy as np
from jax import lax
from jax.experimental import pallas as pl
from jax.experimental.pallas import tpu as pltpu
from jax.sharding import PartitionSpec as P

CELLS = 64
KSIZE = 21
GROUP = 8


gauss_widths = (1.0, 2.0, 3.5)


def band_tables(side_len):
    tap_reach = KSIZE // 2
    position = np.arange(side_len).astype(np.float32)
    offset = position[:, None] - position[None, :]
    inside = np.abs(offset) <= tap_reach
    tap_offsets = np.arange(-tap_reach, tap_reach + 1).astype(np.float32)
    tables = []
    for spread in gauss_widths:
        spread = np.float32(spread)
        width = np.float32(2.0) * spread * spread
        profile_sum = np.sum(np.exp(-tap_offsets * tap_offsets / width), dtype=np.float32)
        even_band = np.where(inside, np.exp(-offset * offset / width) / profile_sum, 0.0)
        even_band = even_band.astype(np.float32)
        tables.append(even_band)
        tables.append((even_band * offset / spread).astype(np.float32))
    return np.stack(tables)


def match_kernel(index_ref, coef_ref, pix_ref, mask_ref, tab_ref, right_ref, out_ref):
    step = pl.program_id(0)
    group, side_len, _ = pix_ref.shape
    bits = mask_ref[...]
    masked = jnp.where((bits & 7) == 0, pix_ref[...], jnp.zeros((), jnp.bfloat16))
    columns = jnp.dot(
        masked.reshape(group * side_len, side_len),
        right_ref[...],
        preferred_element_type=jnp.float32,
    ).astype(jnp.bfloat16)
    for g in range(group):
        chosen = jnp.minimum(jnp.maximum(index_ref[step * group + g], 0), coef_ref.shape[0] // 9 - 1)
        base = chosen * 9
        rows = columns[g * side_len:(g + 1) * side_len]
        acc = jnp.zeros((side_len, side_len), jnp.float32)
        for m in range(3):
            even_band = tab_ref[2 * m]
            odd_band = tab_ref[2 * m + 1]
            left_a = (coef_ref[base + 3 * m] * even_band
                      + coef_ref[base + 3 * m + 1] * odd_band).astype(jnp.bfloat16)
            left_b = (coef_ref[base + 3 * m + 2] * even_band).astype(jnp.bfloat16)
            acc = acc + jnp.dot(
                left_a, rows[:, (2 * m) * side_len:(2 * m + 1) * side_len],
                preferred_element_type=jnp.float32,
            )
            acc = acc + jnp.dot(
                left_b, rows[:, (2 * m + 1) * side_len:(2 * m + 2) * side_len],
                preferred_element_type=jnp.float32,
            )
        out_ref[g] = acc.astype(jnp.bfloat16)


def match_blocks(pixels, mask_bits, coef_index, coef_table, tables, right_bands):
    number, side_len, _ = pixels.shape
    steps = number // GROUP
    flops = number * 4 * side_len * side_len * 6 * side_len
    return pl.pallas_call(
        match_kernel,
        out_shape=jax.ShapeDtypeStruct(pixels.shape, jnp.bfloat16),
        grid=(steps,),
        in_specs=[
            pl.BlockSpec(memory_space=pltpu.SMEM),
            pl.BlockSpec(memory_space=pltpu.SMEM),
            pl.BlockSpec((GROUP, side_len, side_len), lambda i: (i, 0, 0)),
            pl.BlockSpec((GROUP, side_len, side_len), lambda i: (i, 0, 0)),
            pl.BlockSpec(tables.shape, lambda i: (0, 0, 0)),
            pl.BlockSpec(right_bands.shape, lambda i: (0, 0)),
        ],
        out_specs=pl.BlockSpec((GROUP, side_len, side_len), lambda i: (i, 0, 0)),
        cost_estimate=pl.CostEstimate(
            flops=flops, transcendentals=0, bytes_accessed=number * side_len * side_len * 8
        ),
    )(coef_index, coef_table.reshape(-1), pixels, mask_bits, tables, right_bands)


def shards(pixels, mask_bits, inv_var, owner, cell, coef_index, coef_table):
    blocks_here = pixels.shape[0]
    side_len = pixels.shape[1]
    patches = lax.axis_size("patch")
    visits = lax.axis_size("visit")
    devices = patches * visits
    segments = patches * CELLS
    rows_here = side_len // visits
    both = ("visit", "patch")
    tables = band_tables(side_len)
    right_bands = jnp.asarray(
        np.transpose(tables, (2, 0, 1)).reshape(side_len, 6 * side_len), jnp.bfloat16
    )
    tables = jnp.asarray(tables)
    matched_home = match_blocks(pixels, mask_bits, coef_index, coef_table, tables, right_bands)
    meta = jnp.stack([
        inv_var,
        owner.astype(jnp.float32),
        cell.astype(jnp.float32),
        jnp.zeros_like(inv_var),
    ]).astype(jnp.bfloat16).reshape(2, 2 * blocks_here)
    meta = jnp.pad(meta, ((0, 14), (0, side_len - 2 * blocks_here)))
    meta_blocks = jnp.broadcast_to(meta[:, None, :], (16, side_len, side_len))
    payload = jnp.transpose(jnp.concatenate([matched_home, meta_blocks], axis=0), (1, 0, 2))
    received = lax.all_to_all(payload, both, split_axis=0, concat_axis=0, tiled=True)
    row_all = received[:, :blocks_here].reshape(devices * blocks_here, side_len)
    weight_all = received[:, blocks_here, :blocks_here].reshape(-1)
    owner_all = received[:, blocks_here, blocks_here:].reshape(-1).astype(jnp.int32)
    cell_all = received[:, blocks_here + 1, :blocks_here].reshape(-1).astype(jnp.int32)
    segment_all = owner_all * CELLS + cell_all
    picks = segment_all[None, :] == jnp.arange(segments, dtype=jnp.int32)[:, None]
    weighted = jnp.where(picks, weight_all[None, :], jnp.zeros((), jnp.bfloat16))
    numerator = jnp.dot(weighted, row_all, preferred_element_type=jnp.float32)
    owner_pick = (owner_all[None, :] == jnp.arange(patches, dtype=jnp.int32)[:, None]).astype(
        jnp.bfloat16
    )
    cell_pick = jnp.where(
        cell_all[None, :] == jnp.arange(CELLS, dtype=jnp.int32)[:, None],
        weight_all[None, :],
        jnp.zeros((), jnp.bfloat16),
    )
    weight_sum = lax.dot_general(
        owner_pick, cell_pick, (((1,), (1,)), ((), ())), preferred_element_type=jnp.float32
    ).reshape(segments)
    coadd_row = numerator / jnp.maximum(weight_sum, 1.0)[:, None]
    template_row = coadd_row.astype(jnp.bfloat16)
    block_template = lax.dot_general(
        picks.astype(jnp.bfloat16), template_row, (((0,), (0,)), ((), ())),
        preferred_element_type=jnp.float32,
    )
    difference_row = (row_all.astype(jnp.float32) - block_template).astype(jnp.bfloat16)
    returned = lax.all_to_all(
        difference_row.reshape(devices, blocks_here, side_len),
        both, split_axis=0, concat_axis=0, tiled=True,
    )
    difference = jnp.transpose(returned, (1, 0, 2))
    coadd_parts = lax.all_to_all(
        coadd_row.reshape(patches, CELLS, 1, side_len),
        "patch", split_axis=0, concat_axis=2, tiled=True,
    )
    coadd_part = coadd_parts.reshape(CELLS, rows_here, side_len)
    return (coadd_part, difference)


def solution(mesh):
    placed = (
        P(("visit", "patch"), None, None),
        P(("visit", "patch"), None, None),
        P(("visit", "patch")),
        P(("visit", "patch")),
        P(("visit", "patch")),
        P(("visit", "patch")),
        P(),
    )
    return jax.shard_map(
        shards,
        mesh=mesh,
        in_specs=placed,
        out_specs=(P("patch", "visit", None), P(("visit", "patch"), None, None)),
        check_vma=False,
    )
```

```python
import jax
import jax.numpy as jnp
import numpy as np
from jax import lax
from jax.experimental import pallas as pl
from jax.experimental.pallas import tpu as pltpu
from jax.sharding import PartitionSpec as P

CELLS = 64
KSIZE = 21
GROUP = 16


gauss_widths = (1.0, 2.0, 3.5)


def band_tables(side_len):
    tap_reach = KSIZE // 2
    position = np.arange(side_len).astype(np.float32)
    offset = position[:, None] - position[None, :]
    inside = np.abs(offset) <= tap_reach
    tap_offsets = np.arange(-tap_reach, tap_reach + 1).astype(np.float32)
    tables = []
    for spread in gauss_widths:
        spread = np.float32(spread)
        width = np.float32(2.0) * spread * spread
        profile_sum = np.sum(np.exp(-tap_offsets * tap_offsets / width), dtype=np.float32)
        even_band = np.where(inside, np.exp(-offset * offset / width) / profile_sum, 0.0)
        even_band = even_band.astype(np.float32)
        tables.append(even_band)
        tables.append((even_band * offset / spread).astype(np.float32))
    return np.stack(tables)


def match_kernel(index_ref, coef_ref, pix_ref, mask_ref, tab_ref, right_ref, out_ref):
    step = pl.program_id(0)
    group, side_len, _ = pix_ref.shape
    bits = mask_ref[...]
    masked = jnp.where((bits & 7) == 0, pix_ref[...], jnp.zeros((), jnp.bfloat16))
    columns = jnp.dot(
        masked.reshape(group * side_len, side_len),
        right_ref[...],
        preferred_element_type=jnp.float32,
    ).astype(jnp.bfloat16)
    for g in range(group):
        chosen = jnp.minimum(jnp.maximum(index_ref[step * group + g], 0), coef_ref.shape[0] // 9 - 1)
        base = chosen * 9
        rows = columns[g * side_len:(g + 1) * side_len]
        acc = jnp.zeros((side_len, side_len), jnp.float32)
        for m in range(3):
            even_band = tab_ref[2 * m]
            odd_band = tab_ref[2 * m + 1]
            left_a = (coef_ref[base + 3 * m] * even_band
                      + coef_ref[base + 3 * m + 1] * odd_band).astype(jnp.bfloat16)
            left_b = (coef_ref[base + 3 * m + 2] * even_band).astype(jnp.bfloat16)
            acc = acc + jnp.dot(
                left_a, rows[:, (2 * m) * side_len:(2 * m + 1) * side_len],
                preferred_element_type=jnp.float32,
            )
            acc = acc + jnp.dot(
                left_b, rows[:, (2 * m + 1) * side_len:(2 * m + 2) * side_len],
                preferred_element_type=jnp.float32,
            )
        out_ref[g] = acc.astype(jnp.bfloat16)


def match_blocks(pixels, mask_bits, coef_index, coef_table, tables, right_bands):
    number, side_len, _ = pixels.shape
    steps = number // GROUP
    flops = number * 4 * side_len * side_len * 6 * side_len
    return pl.pallas_call(
        match_kernel,
        out_shape=jax.ShapeDtypeStruct(pixels.shape, jnp.bfloat16),
        grid=(steps,),
        in_specs=[
            pl.BlockSpec(memory_space=pltpu.SMEM),
            pl.BlockSpec(memory_space=pltpu.SMEM),
            pl.BlockSpec((GROUP, side_len, side_len), lambda i: (i, 0, 0)),
            pl.BlockSpec((GROUP, side_len, side_len), lambda i: (i, 0, 0)),
            pl.BlockSpec(tables.shape, lambda i: (0, 0, 0)),
            pl.BlockSpec(right_bands.shape, lambda i: (0, 0)),
        ],
        out_specs=pl.BlockSpec((GROUP, side_len, side_len), lambda i: (i, 0, 0)),
        cost_estimate=pl.CostEstimate(
            flops=flops, transcendentals=0, bytes_accessed=number * side_len * side_len * 8
        ),
    )(coef_index, coef_table.reshape(-1), pixels, mask_bits, tables, right_bands)


def shards(pixels, mask_bits, inv_var, owner, cell, coef_index, coef_table):
    blocks_here = pixels.shape[0]
    side_len = pixels.shape[1]
    patches = lax.axis_size("patch")
    visits = lax.axis_size("visit")
    devices = patches * visits
    segments = patches * CELLS
    rows_here = side_len // visits
    both = ("visit", "patch")
    tables = band_tables(side_len)
    right_bands = jnp.asarray(
        np.transpose(tables, (2, 0, 1)).reshape(side_len, 6 * side_len), jnp.bfloat16
    )
    tables = jnp.asarray(tables)
    matched_home = match_blocks(pixels, mask_bits, coef_index, coef_table, tables, right_bands)
    meta = jnp.stack([
        inv_var,
        owner.astype(jnp.float32),
        cell.astype(jnp.float32),
        jnp.zeros_like(inv_var),
    ]).astype(jnp.bfloat16).reshape(2, 2 * blocks_here)
    meta = jnp.pad(meta, ((0, 14), (0, side_len - 2 * blocks_here)))
    meta_blocks = jnp.broadcast_to(meta[:, None, :], (16, side_len, side_len))
    payload = jnp.transpose(jnp.concatenate([matched_home, meta_blocks], axis=0), (1, 0, 2))
    received = lax.all_to_all(payload, both, split_axis=0, concat_axis=0, tiled=True)
    row_all = received[:, :blocks_here].reshape(devices * blocks_here, side_len)
    weight_all = received[:, blocks_here, :blocks_here].reshape(-1)
    owner_all = received[:, blocks_here, blocks_here:].reshape(-1).astype(jnp.int32)
    cell_all = received[:, blocks_here + 1, :blocks_here].reshape(-1).astype(jnp.int32)
    segment_all = owner_all * CELLS + cell_all
    picks = segment_all[None, :] == jnp.arange(segments, dtype=jnp.int32)[:, None]
    weighted = jnp.where(picks, weight_all[None, :], jnp.zeros((), jnp.bfloat16))
    numerator = jnp.dot(weighted, row_all, preferred_element_type=jnp.float32)
    owner_pick = (owner_all[None, :] == jnp.arange(patches, dtype=jnp.int32)[:, None]).astype(
        jnp.bfloat16
    )
    cell_pick = jnp.where(
        cell_all[None, :] == jnp.arange(CELLS, dtype=jnp.int32)[:, None],
        weight_all[None, :],
        jnp.zeros((), jnp.bfloat16),
    )
    weight_sum = lax.dot_general(
        owner_pick, cell_pick, (((1,), (1,)), ((), ())), preferred_element_type=jnp.float32
    ).reshape(segments)
    coadd_row = numerator / jnp.maximum(weight_sum, 1.0)[:, None]
    template_row = coadd_row.astype(jnp.bfloat16)
    block_pick = (
        segment_all[:, None] == jnp.arange(segments, dtype=jnp.int32)[None, :]
    ).astype(jnp.bfloat16)
    block_template = jnp.dot(block_pick, template_row, preferred_element_type=jnp.float32)
    difference_row = (row_all.astype(jnp.float32) - block_template).astype(jnp.bfloat16)
    returned = lax.all_to_all(
        difference_row.reshape(devices, blocks_here, side_len),
        both, split_axis=0, concat_axis=0, tiled=True,
    )
    difference = jnp.transpose(returned, (1, 0, 2))
    coadd_parts = lax.all_to_all(
        coadd_row.reshape(patches, CELLS, 1, side_len),
        "patch", split_axis=0, concat_axis=2, tiled=True,
    )
    coadd_part = coadd_parts.reshape(CELLS, rows_here, side_len)
    return (coadd_part, difference)


def solution(mesh):
    placed = (
        P(("visit", "patch"), None, None),
        P(("visit", "patch"), None, None),
        P(("visit", "patch")),
        P(("visit", "patch")),
        P(("visit", "patch")),
        P(("visit", "patch")),
        P(),
    )
    return jax.shard_map(
        shards,
        mesh=mesh,
        in_specs=placed,
        out_specs=(P("patch", "visit", None), P(("visit", "patch"), None, None)),
        check_vma=False,
    )
```

```python
import jax
import jax.numpy as jnp
import numpy as np
from jax import lax
from jax.experimental import pallas as pl
from jax.experimental.pallas import tpu as pltpu
from jax.sharding import PartitionSpec as P

CELLS = 64
KSIZE = 21
GROUP = 16


gauss_widths = (1.0, 2.0, 3.5)


def band_tables(side_len):
    tap_reach = KSIZE // 2
    position = np.arange(side_len).astype(np.float32)
    offset = position[:, None] - position[None, :]
    inside = np.abs(offset) <= tap_reach
    tap_offsets = np.arange(-tap_reach, tap_reach + 1).astype(np.float32)
    tables = []
    for spread in gauss_widths:
        spread = np.float32(spread)
        width = np.float32(2.0) * spread * spread
        profile_sum = np.sum(np.exp(-tap_offsets * tap_offsets / width), dtype=np.float32)
        even_band = np.where(inside, np.exp(-offset * offset / width) / profile_sum, 0.0)
        even_band = even_band.astype(np.float32)
        tables.append(even_band)
        tables.append((even_band * offset / spread).astype(np.float32))
    return np.stack(tables)


def match_kernel(index_ref, coef_ref, pix_ref, mask_ref, tab_ref, right_ref, out_ref):
    step = pl.program_id(0)
    group, side_len, _ = pix_ref.shape
    bits = mask_ref[...]
    masked = jnp.where(
        (bits & 7) == 0, pix_ref[...].astype(jnp.float32), jnp.zeros((), jnp.float32)
    ).astype(jnp.bfloat16)
    columns = jnp.dot(
        masked.reshape(group * side_len, side_len),
        right_ref[...],
        preferred_element_type=jnp.float32,
    ).astype(jnp.bfloat16)
    for g in range(group):
        chosen = jnp.minimum(jnp.maximum(index_ref[step * group + g], 0), coef_ref.shape[0] // 9 - 1)
        base = chosen * 9
        rows = columns[g * side_len:(g + 1) * side_len]
        acc = jnp.zeros((side_len, side_len), jnp.float32)
        for m in range(3):
            even_band = tab_ref[2 * m]
            odd_band = tab_ref[2 * m + 1]
            left_a = (coef_ref[base + 3 * m] * even_band
                      + coef_ref[base + 3 * m + 1] * odd_band).astype(jnp.bfloat16)
            left_b = (coef_ref[base + 3 * m + 2] * even_band).astype(jnp.bfloat16)
            acc = acc + jnp.dot(
                left_a, rows[:, (2 * m) * side_len:(2 * m + 1) * side_len],
                preferred_element_type=jnp.float32,
            )
            acc = acc + jnp.dot(
                left_b, rows[:, (2 * m + 1) * side_len:(2 * m + 2) * side_len],
                preferred_element_type=jnp.float32,
            )
        out_ref[g] = acc.astype(jnp.bfloat16)


def match_blocks(pixels, mask_bits, coef_index, coef_table, tables, right_bands):
    number, side_len, _ = pixels.shape
    steps = number // GROUP
    flops = number * 4 * side_len * side_len * 6 * side_len
    return pl.pallas_call(
        match_kernel,
        out_shape=jax.ShapeDtypeStruct(pixels.shape, jnp.bfloat16),
        grid=(steps,),
        in_specs=[
            pl.BlockSpec(memory_space=pltpu.SMEM),
            pl.BlockSpec(memory_space=pltpu.SMEM),
            pl.BlockSpec((GROUP, side_len, side_len), lambda i: (i, 0, 0)),
            pl.BlockSpec((GROUP, side_len, side_len), lambda i: (i, 0, 0)),
            pl.BlockSpec(tables.shape, lambda i: (0, 0, 0)),
            pl.BlockSpec(right_bands.shape, lambda i: (0, 0)),
        ],
        out_specs=pl.BlockSpec((GROUP, side_len, side_len), lambda i: (i, 0, 0)),
        cost_estimate=pl.CostEstimate(
            flops=flops, transcendentals=0, bytes_accessed=number * side_len * side_len * 8
        ),
    )(coef_index, coef_table.reshape(-1), pixels, mask_bits, tables, right_bands)


def shards(pixels, mask_bits, inv_var, owner, cell, coef_index, coef_table):
    blocks_here = pixels.shape[0]
    side_len = pixels.shape[1]
    patches = lax.axis_size("patch")
    visits = lax.axis_size("visit")
    devices = patches * visits
    segments = patches * CELLS
    rows_here = side_len // visits
    both = ("visit", "patch")
    tables = band_tables(side_len)
    right_bands = jnp.asarray(
        np.transpose(tables, (2, 0, 1)).reshape(side_len, 6 * side_len), jnp.bfloat16
    )
    tables = jnp.asarray(tables)
    matched_home = match_blocks(pixels, mask_bits, coef_index, coef_table, tables, right_bands)
    meta = jnp.stack([
        inv_var,
        owner.astype(jnp.float32),
        cell.astype(jnp.float32),
        jnp.zeros_like(inv_var),
    ]).astype(jnp.bfloat16).reshape(2, 2 * blocks_here)
    meta = jnp.pad(meta, ((0, 14), (0, side_len - 2 * blocks_here)))
    meta_blocks = jnp.broadcast_to(meta[:, None, :], (16, side_len, side_len))
    payload = jnp.transpose(jnp.concatenate([matched_home, meta_blocks], axis=0), (1, 0, 2))
    received = lax.all_to_all(payload, both, split_axis=0, concat_axis=0, tiled=True)
    row_all = received[:, :blocks_here].reshape(devices * blocks_here, side_len)
    weight_all = received[:, blocks_here, :blocks_here].reshape(-1)
    owner_all = received[:, blocks_here, blocks_here:].reshape(-1).astype(jnp.int32)
    cell_all = received[:, blocks_here + 1, :blocks_here].reshape(-1).astype(jnp.int32)
    segment_all = owner_all * CELLS + cell_all
    picks = segment_all[None, :] == jnp.arange(segments, dtype=jnp.int32)[:, None]
    weighted = jnp.where(picks, weight_all[None, :], jnp.zeros((), jnp.bfloat16))
    numerator = jnp.dot(weighted, row_all, preferred_element_type=jnp.float32)
    owner_pick = (owner_all[None, :] == jnp.arange(patches, dtype=jnp.int32)[:, None]).astype(
        jnp.bfloat16
    )
    cell_pick = jnp.where(
        cell_all[None, :] == jnp.arange(CELLS, dtype=jnp.int32)[:, None],
        weight_all[None, :],
        jnp.zeros((), jnp.bfloat16),
    )
    weight_sum = lax.dot_general(
        owner_pick, cell_pick, (((1,), (1,)), ((), ())), preferred_element_type=jnp.float32
    ).reshape(segments)
    coadd_row = numerator / jnp.maximum(weight_sum, 1.0)[:, None]
    template_row = coadd_row.astype(jnp.bfloat16)
    block_pick = (
        segment_all[:, None] == jnp.arange(segments, dtype=jnp.int32)[None, :]
    ).astype(jnp.bfloat16)
    block_template = jnp.dot(block_pick, template_row, preferred_element_type=jnp.float32)
    difference_row = (row_all.astype(jnp.float32) - block_template).astype(jnp.bfloat16)
    returned = lax.all_to_all(
        difference_row.reshape(devices, blocks_here, side_len),
        both, split_axis=0, concat_axis=0, tiled=True,
    )
    difference = jnp.transpose(returned, (1, 0, 2))
    coadd_parts = lax.all_to_all(
        coadd_row.reshape(patches, CELLS, 1, side_len),
        "patch", split_axis=0, concat_axis=2, tiled=True,
    )
    coadd_part = coadd_parts.reshape(CELLS, rows_here, side_len)
    return (coadd_part, difference)


def solution(mesh):
    placed = (
        P(("visit", "patch"), None, None),
        P(("visit", "patch"), None, None),
        P(("visit", "patch")),
        P(("visit", "patch")),
        P(("visit", "patch")),
        P(("visit", "patch")),
        P(),
    )
    return jax.shard_map(
        shards,
        mesh=mesh,
        in_specs=placed,
        out_specs=(P("patch", "visit", None), P(("visit", "patch"), None, None)),
        check_vma=False,
    )
```

```python
import jax
import jax.numpy as jnp
import numpy as np
from jax import lax
from jax.experimental import pallas as pl
from jax.experimental.pallas import tpu as pltpu
from jax.sharding import PartitionSpec as P

CELLS = 64
KSIZE = 21
GROUP = 16


gauss_widths = (1.0, 2.0, 3.5)


def band_tables(side_len):
    tap_reach = KSIZE // 2
    position = np.arange(side_len).astype(np.float32)
    offset = position[:, None] - position[None, :]
    inside = np.abs(offset) <= tap_reach
    tap_offsets = np.arange(-tap_reach, tap_reach + 1).astype(np.float32)
    tables = []
    for spread in gauss_widths:
        spread = np.float32(spread)
        width = np.float32(2.0) * spread * spread
        profile_sum = np.sum(np.exp(-tap_offsets * tap_offsets / width), dtype=np.float32)
        even_band = np.where(inside, np.exp(-offset * offset / width) / profile_sum, 0.0)
        even_band = even_band.astype(np.float32)
        tables.append(even_band)
        tables.append((even_band * offset / spread).astype(np.float32))
    return np.stack(tables)


def match_kernel(index_ref, coef_ref, pix_ref, mask_ref, tab_ref, right_ref, out_ref):
    step = pl.program_id(0)
    group, side_len, _ = pix_ref.shape
    bits = mask_ref[...]
    masked = jnp.where((bits & 7) == 0, pix_ref[...], jnp.zeros((), jnp.bfloat16))
    columns = jnp.dot(
        masked.reshape(group * side_len, side_len),
        right_ref[...],
        preferred_element_type=jnp.float32,
    ).astype(jnp.bfloat16)
    for g in range(group):
        chosen = jnp.minimum(jnp.maximum(index_ref[step * group + g], 0), coef_ref.shape[0] // 9 - 1)
        base = chosen * 9
        rows = columns[g * side_len:(g + 1) * side_len]
        acc = jnp.zeros((side_len, side_len), jnp.float32)
        for m in range(3):
            even_band = tab_ref[2 * m]
            odd_band = tab_ref[2 * m + 1]
            left_a = (coef_ref[base + 3 * m] * even_band
                      + coef_ref[base + 3 * m + 1] * odd_band).astype(jnp.bfloat16)
            left_b = (coef_ref[base + 3 * m + 2] * even_band).astype(jnp.bfloat16)
            acc = acc + jnp.dot(
                left_a, rows[:, (2 * m) * side_len:(2 * m + 1) * side_len],
                preferred_element_type=jnp.float32,
            )
            acc = acc + jnp.dot(
                left_b, rows[:, (2 * m + 1) * side_len:(2 * m + 2) * side_len],
                preferred_element_type=jnp.float32,
            )
        out_ref[:, pl.ds(g, 1), :] = acc.astype(jnp.bfloat16)[:, None, :]


def match_blocks(pixels, mask_bits, coef_index, coef_table, tables, right_bands):
    number, side_len, _ = pixels.shape
    steps = number // GROUP
    flops = number * 4 * side_len * side_len * 6 * side_len
    return pl.pallas_call(
        match_kernel,
        out_shape=jax.ShapeDtypeStruct((side_len, number, side_len), jnp.bfloat16),
        grid=(steps,),
        in_specs=[
            pl.BlockSpec(memory_space=pltpu.SMEM),
            pl.BlockSpec(memory_space=pltpu.SMEM),
            pl.BlockSpec((GROUP, side_len, side_len), lambda i: (i, 0, 0)),
            pl.BlockSpec((GROUP, side_len, side_len), lambda i: (i, 0, 0)),
            pl.BlockSpec(tables.shape, lambda i: (0, 0, 0)),
            pl.BlockSpec(right_bands.shape, lambda i: (0, 0)),
        ],
        out_specs=pl.BlockSpec((side_len, GROUP, side_len), lambda i: (0, i, 0)),
        cost_estimate=pl.CostEstimate(
            flops=flops, transcendentals=0, bytes_accessed=number * side_len * side_len * 8
        ),
    )(coef_index, coef_table.reshape(-1), pixels, mask_bits, tables, right_bands)


def shards(pixels, mask_bits, inv_var, owner, cell, coef_index, coef_table):
    blocks_here = pixels.shape[0]
    side_len = pixels.shape[1]
    patches = lax.axis_size("patch")
    visits = lax.axis_size("visit")
    devices = patches * visits
    segments = patches * CELLS
    rows_here = side_len // visits
    both = ("visit", "patch")
    tables = band_tables(side_len)
    right_bands = jnp.asarray(
        np.transpose(tables, (2, 0, 1)).reshape(side_len, 6 * side_len), jnp.bfloat16
    )
    tables = jnp.asarray(tables)
    matched_home = match_blocks(pixels, mask_bits, coef_index, coef_table, tables, right_bands)
    meta = jnp.stack([
        inv_var,
        owner.astype(jnp.float32),
        cell.astype(jnp.float32),
        jnp.zeros_like(inv_var),
    ]).astype(jnp.bfloat16).reshape(2, 2 * blocks_here)
    meta = jnp.pad(meta, ((0, 14), (0, side_len - 2 * blocks_here)))
    meta_blocks = jnp.broadcast_to(meta[:, None, :], (16, side_len, side_len))
    payload = jnp.concatenate([matched_home, jnp.transpose(meta_blocks, (1, 0, 2))], axis=1)
    received = lax.all_to_all(payload, both, split_axis=0, concat_axis=0, tiled=True)
    row_all = received[:, :blocks_here].reshape(devices * blocks_here, side_len)
    weight_all = received[:, blocks_here, :blocks_here].reshape(-1)
    owner_all = received[:, blocks_here, blocks_here:].reshape(-1).astype(jnp.int32)
    cell_all = received[:, blocks_here + 1, :blocks_here].reshape(-1).astype(jnp.int32)
    segment_all = owner_all * CELLS + cell_all
    picks = segment_all[None, :] == jnp.arange(segments, dtype=jnp.int32)[:, None]
    weighted = jnp.where(picks, weight_all[None, :], jnp.zeros((), jnp.bfloat16))
    numerator = jnp.dot(weighted, row_all, preferred_element_type=jnp.float32)
    owner_pick = (owner_all[None, :] == jnp.arange(patches, dtype=jnp.int32)[:, None]).astype(
        jnp.bfloat16
    )
    cell_pick = jnp.where(
        cell_all[None, :] == jnp.arange(CELLS, dtype=jnp.int32)[:, None],
        weight_all[None, :],
        jnp.zeros((), jnp.bfloat16),
    )
    weight_sum = lax.dot_general(
        owner_pick, cell_pick, (((1,), (1,)), ((), ())), preferred_element_type=jnp.float32
    ).reshape(segments)
    coadd_row = numerator / jnp.maximum(weight_sum, 1.0)[:, None]
    template_row = coadd_row.astype(jnp.bfloat16)
    block_pick = (
        segment_all[:, None] == jnp.arange(segments, dtype=jnp.int32)[None, :]
    ).astype(jnp.bfloat16)
    block_template = jnp.dot(block_pick, template_row, preferred_element_type=jnp.float32)
    difference_row = (row_all.astype(jnp.float32) - block_template).astype(jnp.bfloat16)
    returned = lax.all_to_all(
        difference_row.reshape(devices, blocks_here, side_len),
        both, split_axis=0, concat_axis=0, tiled=True,
    )
    difference = jnp.transpose(returned, (1, 0, 2))
    coadd_parts = lax.all_to_all(
        coadd_row.reshape(patches, CELLS, 1, side_len),
        "patch", split_axis=0, concat_axis=2, tiled=True,
    )
    coadd_part = coadd_parts.reshape(CELLS, rows_here, side_len)
    return (coadd_part, difference)


def solution(mesh):
    placed = (
        P(("visit", "patch"), None, None),
        P(("visit", "patch"), None, None),
        P(("visit", "patch")),
        P(("visit", "patch")),
        P(("visit", "patch")),
        P(("visit", "patch")),
        P(),
    )
    return jax.shard_map(
        shards,
        mesh=mesh,
        in_specs=placed,
        out_specs=(P("patch", "visit", None), P(("visit", "patch"), None, None)),
        check_vma=False,
    )
```

```python
import jax
import jax.numpy as jnp
import numpy as np
from jax import lax
from jax.experimental import pallas as pl
from jax.experimental.pallas import tpu as pltpu
from jax.sharding import PartitionSpec as P

CELLS = 64
KSIZE = 21
GROUP = 32


gauss_widths = (1.0, 2.0, 3.5)


def band_tables(side_len):
    tap_reach = KSIZE // 2
    position = np.arange(side_len).astype(np.float32)
    offset = position[:, None] - position[None, :]
    inside = np.abs(offset) <= tap_reach
    tap_offsets = np.arange(-tap_reach, tap_reach + 1).astype(np.float32)
    tables = []
    for spread in gauss_widths:
        spread = np.float32(spread)
        width = np.float32(2.0) * spread * spread
        profile_sum = np.sum(np.exp(-tap_offsets * tap_offsets / width), dtype=np.float32)
        even_band = np.where(inside, np.exp(-offset * offset / width) / profile_sum, 0.0)
        even_band = even_band.astype(np.float32)
        tables.append(even_band)
        tables.append((even_band * offset / spread).astype(np.float32))
    return np.stack(tables)


def match_kernel(index_ref, coef_ref, pix_ref, mask_ref, tab_ref, right_ref, out_ref):
    step = pl.program_id(0)
    group, side_len, _ = pix_ref.shape
    bits = mask_ref[...]
    masked = jnp.where((bits & 7) == 0, pix_ref[...], jnp.zeros((), jnp.bfloat16))
    columns = jnp.dot(
        masked.reshape(group * side_len, side_len),
        right_ref[...],
        preferred_element_type=jnp.float32,
    ).astype(jnp.bfloat16)
    for g in range(group):
        chosen = jnp.minimum(jnp.maximum(index_ref[step * group + g], 0), coef_ref.shape[0] // 9 - 1)
        base = chosen * 9
        rows = columns[g * side_len:(g + 1) * side_len]
        acc = jnp.zeros((side_len, side_len), jnp.float32)
        for m in range(3):
            even_band = tab_ref[2 * m]
            odd_band = tab_ref[2 * m + 1]
            left_a = (coef_ref[base + 3 * m] * even_band
                      + coef_ref[base + 3 * m + 1] * odd_band).astype(jnp.bfloat16)
            left_b = (coef_ref[base + 3 * m + 2] * even_band).astype(jnp.bfloat16)
            acc = acc + jnp.dot(
                left_a, rows[:, (2 * m) * side_len:(2 * m + 1) * side_len],
                preferred_element_type=jnp.float32,
            )
            acc = acc + jnp.dot(
                left_b, rows[:, (2 * m + 1) * side_len:(2 * m + 2) * side_len],
                preferred_element_type=jnp.float32,
            )
        out_ref[g] = acc.astype(jnp.bfloat16)


def match_blocks(pixels, mask_bits, coef_index, coef_table, tables, right_bands):
    number, side_len, _ = pixels.shape
    steps = number // GROUP
    flops = number * 4 * side_len * side_len * 6 * side_len
    return pl.pallas_call(
        match_kernel,
        out_shape=jax.ShapeDtypeStruct(pixels.shape, jnp.bfloat16),
        grid=(steps,),
        in_specs=[
            pl.BlockSpec(memory_space=pltpu.SMEM),
            pl.BlockSpec(memory_space=pltpu.SMEM),
            pl.BlockSpec((GROUP, side_len, side_len), lambda i: (i, 0, 0)),
            pl.BlockSpec((GROUP, side_len, side_len), lambda i: (i, 0, 0)),
            pl.BlockSpec(tables.shape, lambda i: (0, 0, 0)),
            pl.BlockSpec(right_bands.shape, lambda i: (0, 0)),
        ],
        out_specs=pl.BlockSpec((GROUP, side_len, side_len), lambda i: (i, 0, 0)),
        cost_estimate=pl.CostEstimate(
            flops=flops, transcendentals=0, bytes_accessed=number * side_len * side_len * 8
        ),
    )(coef_index, coef_table.reshape(-1), pixels, mask_bits, tables, right_bands)


def shards(pixels, mask_bits, inv_var, owner, cell, coef_index, coef_table):
    blocks_here = pixels.shape[0]
    side_len = pixels.shape[1]
    patches = lax.axis_size("patch")
    visits = lax.axis_size("visit")
    devices = patches * visits
    segments = patches * CELLS
    rows_here = side_len // visits
    both = ("visit", "patch")
    tables = band_tables(side_len)
    right_bands = jnp.asarray(
        np.transpose(tables, (2, 0, 1)).reshape(side_len, 6 * side_len), jnp.bfloat16
    )
    tables = jnp.asarray(tables)
    matched_home = match_blocks(pixels, mask_bits, coef_index, coef_table, tables, right_bands)
    meta = jnp.stack([
        inv_var,
        owner.astype(jnp.float32),
        cell.astype(jnp.float32),
        jnp.zeros_like(inv_var),
    ]).astype(jnp.bfloat16).reshape(2, 2 * blocks_here)
    meta = jnp.pad(meta, ((0, 14), (0, side_len - 2 * blocks_here)))
    meta_blocks = jnp.broadcast_to(meta[:, None, :], (16, side_len, side_len))
    payload = jnp.transpose(jnp.concatenate([matched_home, meta_blocks], axis=0), (1, 0, 2))
    received = lax.all_to_all(payload, both, split_axis=0, concat_axis=0, tiled=True)
    row_all = received[:, :blocks_here].reshape(devices * blocks_here, side_len)
    weight_all = received[:, blocks_here, :blocks_here].reshape(-1)
    owner_all = received[:, blocks_here, blocks_here:].reshape(-1).astype(jnp.int32)
    cell_all = received[:, blocks_here + 1, :blocks_here].reshape(-1).astype(jnp.int32)
    segment_all = owner_all * CELLS + cell_all
    picks = segment_all[None, :] == jnp.arange(segments, dtype=jnp.int32)[:, None]
    weighted = jnp.where(picks, weight_all[None, :], jnp.zeros((), jnp.bfloat16))
    numerator = jnp.dot(weighted, row_all, preferred_element_type=jnp.float32)
    owner_pick = (owner_all[None, :] == jnp.arange(patches, dtype=jnp.int32)[:, None]).astype(
        jnp.bfloat16
    )
    cell_pick = jnp.where(
        cell_all[None, :] == jnp.arange(CELLS, dtype=jnp.int32)[:, None],
        weight_all[None, :],
        jnp.zeros((), jnp.bfloat16),
    )
    weight_sum = lax.dot_general(
        owner_pick, cell_pick, (((1,), (1,)), ((), ())), preferred_element_type=jnp.float32
    ).reshape(segments)
    coadd_row = numerator / jnp.maximum(weight_sum, 1.0)[:, None]
    template_row = coadd_row.astype(jnp.bfloat16)
    block_pick = (
        segment_all[:, None] == jnp.arange(segments, dtype=jnp.int32)[None, :]
    ).astype(jnp.bfloat16)
    block_template = jnp.dot(block_pick, template_row, preferred_element_type=jnp.float32)
    difference_row = (row_all.astype(jnp.float32) - block_template).astype(jnp.bfloat16)
    returned = lax.all_to_all(
        difference_row.reshape(devices, blocks_here, side_len),
        both, split_axis=0, concat_axis=0, tiled=True,
    )
    difference = jnp.transpose(returned, (1, 0, 2))
    coadd_parts = lax.all_to_all(
        coadd_row.reshape(patches, CELLS, 1, side_len),
        "patch", split_axis=0, concat_axis=2, tiled=True,
    )
    coadd_part = coadd_parts.reshape(CELLS, rows_here, side_len)
    return (coadd_part, difference)


def solution(mesh):
    placed = (
        P(("visit", "patch"), None, None),
        P(("visit", "patch"), None, None),
        P(("visit", "patch")),
        P(("visit", "patch")),
        P(("visit", "patch")),
        P(("visit", "patch")),
        P(),
    )
    return jax.shard_map(
        shards,
        mesh=mesh,
        in_specs=placed,
        out_specs=(P("patch", "visit", None), P(("visit", "patch"), None, None)),
        check_vma=False,
    )
```

```python
import jax
import jax.numpy as jnp
import numpy as np
from jax import lax
from jax.experimental import pallas as pl
from jax.experimental.pallas import tpu as pltpu
from jax.sharding import PartitionSpec as P

CELLS = 64
KSIZE = 21
GROUP = 16


gauss_widths = (1.0, 2.0, 3.5)


def band_tables(side_len):
    tap_reach = KSIZE // 2
    position = np.arange(side_len).astype(np.float32)
    offset = position[:, None] - position[None, :]
    inside = np.abs(offset) <= tap_reach
    tap_offsets = np.arange(-tap_reach, tap_reach + 1).astype(np.float32)
    tables = []
    for spread in gauss_widths:
        spread = np.float32(spread)
        width = np.float32(2.0) * spread * spread
        profile_sum = np.sum(np.exp(-tap_offsets * tap_offsets / width), dtype=np.float32)
        even_band = np.where(inside, np.exp(-offset * offset / width) / profile_sum, 0.0)
        even_band = even_band.astype(np.float32)
        tables.append(even_band)
        tables.append((even_band * offset / spread).astype(np.float32))
    return np.stack(tables)


def match_kernel(index_ref, coef_ref, pix_ref, mask_ref, tab_ref, right_ref, out_ref):
    step = pl.program_id(0)
    group, side_len, _ = pix_ref.shape
    bits = mask_ref[...]
    masked = jnp.where((bits & 7) == 0, pix_ref[...], jnp.zeros((), jnp.bfloat16))
    columns = jnp.dot(
        masked.reshape(group * side_len, side_len),
        right_ref[...],
        preferred_element_type=jnp.float32,
    ).astype(jnp.bfloat16)
    for g in range(group):
        chosen = jnp.minimum(jnp.maximum(index_ref[step * group + g], 0), coef_ref.shape[0] // 9 - 1)
        base = chosen * 9
        rows = columns[g * side_len:(g + 1) * side_len]
        acc = jnp.zeros((side_len, side_len), jnp.float32)
        for m in range(3):
            even_band = tab_ref[2 * m]
            odd_band = tab_ref[2 * m + 1]
            left_a = (coef_ref[base + 3 * m] * even_band
                      + coef_ref[base + 3 * m + 1] * odd_band).astype(jnp.bfloat16)
            left_b = (coef_ref[base + 3 * m + 2] * even_band).astype(jnp.bfloat16)
            acc = acc + jnp.dot(
                left_a, rows[:, (2 * m) * side_len:(2 * m + 1) * side_len],
                preferred_element_type=jnp.float32,
            )
            acc = acc + jnp.dot(
                left_b, rows[:, (2 * m + 1) * side_len:(2 * m + 2) * side_len],
                preferred_element_type=jnp.float32,
            )
        out_ref[g] = acc.astype(jnp.bfloat16)


def match_blocks(pixels, mask_bits, coef_index, coef_table, tables, right_bands):
    number, side_len, _ = pixels.shape
    steps = number // GROUP
    flops = number * 4 * side_len * side_len * 6 * side_len
    return pl.pallas_call(
        match_kernel,
        out_shape=jax.ShapeDtypeStruct(pixels.shape, jnp.bfloat16),
        grid=(steps,),
        in_specs=[
            pl.BlockSpec(memory_space=pltpu.SMEM),
            pl.BlockSpec(memory_space=pltpu.SMEM),
            pl.BlockSpec((GROUP, side_len, side_len), lambda i: (i, 0, 0)),
            pl.BlockSpec((GROUP, side_len, side_len), lambda i: (i, 0, 0)),
            pl.BlockSpec(tables.shape, lambda i: (0, 0, 0)),
            pl.BlockSpec(right_bands.shape, lambda i: (0, 0)),
        ],
        out_specs=pl.BlockSpec((GROUP, side_len, side_len), lambda i: (i, 0, 0)),
        cost_estimate=pl.CostEstimate(
            flops=flops, transcendentals=0, bytes_accessed=number * side_len * side_len * 8
        ),
    )(coef_index, coef_table.reshape(-1), pixels, mask_bits, tables, right_bands)


def shards(pixels, mask_bits, inv_var, owner, cell, coef_index, coef_table):
    blocks_here = pixels.shape[0]
    side_len = pixels.shape[1]
    patches = lax.axis_size("patch")
    visits = lax.axis_size("visit")
    devices = patches * visits
    segments = patches * CELLS
    rows_here = side_len // visits
    both = ("visit", "patch")
    tables = band_tables(side_len)
    right_bands = jnp.asarray(
        np.transpose(tables, (2, 0, 1)).reshape(side_len, 6 * side_len), jnp.bfloat16
    )
    tables = jnp.asarray(tables)
    matched_home = match_blocks(pixels, mask_bits, coef_index, coef_table, tables, right_bands)
    meta = jnp.stack([
        inv_var,
        owner.astype(jnp.float32),
        cell.astype(jnp.float32),
        jnp.zeros_like(inv_var),
    ]).astype(jnp.bfloat16).reshape(2, 2 * blocks_here)
    meta = jnp.pad(meta, ((0, 14), (0, side_len - 2 * blocks_here)))
    meta_blocks = jnp.broadcast_to(meta[:, None, :], (16, side_len, side_len))
    payload = jnp.transpose(jnp.concatenate([matched_home, meta_blocks], axis=0), (1, 0, 2))
    received = lax.all_to_all(payload, both, split_axis=0, concat_axis=0, tiled=True)
    row_all = received[:, :blocks_here].reshape(devices * blocks_here, side_len)
    weight_all = received[:, blocks_here, :blocks_here].reshape(-1)
    owner_code = received[:, blocks_here, blocks_here:].reshape(-1)
    cell_code = received[:, blocks_here + 1, :blocks_here].reshape(-1)
    owner_all = owner_code.astype(jnp.int32)
    cell_all = cell_code.astype(jnp.int32)
    segment_owner = (jnp.arange(segments) // CELLS).astype(jnp.bfloat16)
    segment_cell = (jnp.arange(segments) % CELLS).astype(jnp.bfloat16)
    picks = (owner_code[None, :] == segment_owner[:, None]) & (
        cell_code[None, :] == segment_cell[:, None]
    )
    weighted = jnp.where(picks, weight_all[None, :], jnp.zeros((), jnp.bfloat16))
    numerator = jnp.dot(weighted, row_all, preferred_element_type=jnp.float32)
    owner_pick = (owner_all[None, :] == jnp.arange(patches, dtype=jnp.int32)[:, None]).astype(
        jnp.bfloat16
    )
    cell_pick = jnp.where(
        cell_all[None, :] == jnp.arange(CELLS, dtype=jnp.int32)[:, None],
        weight_all[None, :],
        jnp.zeros((), jnp.bfloat16),
    )
    weight_sum = lax.dot_general(
        owner_pick, cell_pick, (((1,), (1,)), ((), ())), preferred_element_type=jnp.float32
    ).reshape(segments)
    coadd_row = numerator / jnp.maximum(weight_sum, 1.0)[:, None]
    template_row = coadd_row.astype(jnp.bfloat16)
    block_pick = (
        (owner_code[:, None] == segment_owner[None, :])
        & (cell_code[:, None] == segment_cell[None, :])
    ).astype(jnp.bfloat16)
    block_template = jnp.dot(block_pick, template_row, preferred_element_type=jnp.float32)
    difference_row = (row_all.astype(jnp.float32) - block_template).astype(jnp.bfloat16)
    returned = lax.all_to_all(
        difference_row.reshape(devices, blocks_here, side_len),
        both, split_axis=0, concat_axis=0, tiled=True,
    )
    difference = jnp.transpose(returned, (1, 0, 2))
    coadd_parts = lax.all_to_all(
        coadd_row.reshape(patches, CELLS, 1, side_len),
        "patch", split_axis=0, concat_axis=2, tiled=True,
    )
    coadd_part = coadd_parts.reshape(CELLS, rows_here, side_len)
    return (coadd_part, difference)


def solution(mesh):
    placed = (
        P(("visit", "patch"), None, None),
        P(("visit", "patch"), None, None),
        P(("visit", "patch")),
        P(("visit", "patch")),
        P(("visit", "patch")),
        P(("visit", "patch")),
        P(),
    )
    return jax.shard_map(
        shards,
        mesh=mesh,
        in_specs=placed,
        out_specs=(P("patch", "visit", None), P(("visit", "patch"), None, None)),
        check_vma=False,
    )
```
